768 devices in a mesh: gx: 24 (over z, y_lo), gy: 32 (over y_hi, x, core).
Axes of the slice: x: 4, y: 8 (y_hi: 4, y_lo: 2; y = y_hi * 2 + y_lo), z: 12, core: 2. Of those that a mesh axis runs over, the one named last changes fastest.
Arguments:
- winds: float32 [3, 28, 192, 4096], P(None, None, 'gx', 'gy'), may hold values from -6 to 6
- thermo: float32 [3, 28, 192, 4096], P(None, None, 'gx', 'gy'), may hold values from -6 to 6
- terrain: float32 [192, 4096], P('gx', 'gy'), may hold values from 0 to 2
- shadow_len: int32 [4096], P('gy'), may hold values from 1 to 4
- sector: int32 [4096], P('gy'), may hold values from 0 to 1
- land_mask: int32 [24, 32], P('gx', 'gy'), may hold values from 0 to 1
Outputs:
- winds_out: float32 [3, 28, 192, 4096], P(None, None, 'gx', 'gy')
- thermo_out: float32 [3, 28, 192, 4096], P(None, None, 'gx', 'gy')
The draws below stay inside these ranges and needn't reach their ends.
Inputs may be any that keep to these rules, and one draw needn't show every extreme that they name: `shadow_len`: every row reaches at least one tile; the longest reach is 4 tiles.
All inputs are finite; a program needn't handle non-finite values.
Results may differ from the reference program's by a relative error of at most 0.00002.
Values sent between devices are 32-bit elements; how exact they have to be, the bound alone decides.
No kernel may reach another device: no remote copies, remote signals or barrier semaphores. Data moves between devices by JAX's collectives and lax.ppermute only.
A program may use at most 32 MiB of HBM per device.

```python
import jax
import jax.numpy as jnp

K = 28
CX = 8
CY = 128
ITERS = 2
LMAX = 4
NX = 192
NY = 4096
N_GX = 24
N_GY = 32


def plant(entries, rng, least, top_value):
    longest = entries.shape.index(max(entries.shape))
    spots = []
    for shift in (0, 1):
        where = [jax.random.randint(jax.random.fold_in(rng, axis), (), 0, length) for axis, length in enumerate(entries.shape)]
        where[longest] = (where[longest] + shift) % entries.shape[longest]
        spots.append(tuple(where))
    return entries.at[spots[0]].set(least).at[spots[1]].set(top_value)


def steps_of(rng, shape, split, least, largest):
    level, own = 1.0, jax.random.fold_in(rng, 6)
    for dim, blocks in split:
        steps = jnp.exp(jax.random.uniform(jax.random.fold_in(own, dim), (blocks,), jnp.float32, least / len(split), largest / len(split)))
        level = level * jnp.repeat(steps, shape[dim] // blocks).reshape([-1 if axis == dim else 1 for axis in range(len(shape))])
    return level


def normal_values(key, shape, width, bound, split=(), dtype=jnp.bfloat16):
    factor_of = steps_of(key, shape, split, -0.22, 0.18) if split else 1.0
    array = jax.random.normal(key, shape, jnp.float32) * width * factor_of
    return jnp.minimum(jnp.maximum(array, -bound), bound).astype(dtype)


def setup_inputs(seed: int = 0) -> dict:
    seeds = jax.random.split(jax.random.key(seed), 7)
    return {
        "winds": normal_values(seeds[0], (3, K, NX, NY), 1.0, 6.0, ((2, 24), (3, 32)), jnp.float32),
        "thermo": normal_values(seeds[1], (3, K, NX, NY), 1.0, 6.0, ((2, 24), (3, 32)), jnp.float32),
        "terrain": jnp.clip(2.0 * jax.random.uniform(seeds[2], (NX, NY), jnp.float32) ** steps_of(seeds[2], (NX, NY), ((0, 24), (1, 32)), -0.2, 0.2), 0.0, 2.0),
        "shadow_len": plant(jax.random.randint(seeds[3], (NY,), 1, LMAX + 1), jax.random.fold_in(seeds[3], 1), 1, LMAX).astype(jnp.int32),
        "sector": plant(jax.random.randint(seeds[4], (NY,), 0, 2), jax.random.fold_in(seeds[4], 1), 0, 1).astype(jnp.int32),
        "land_mask": plant(jax.random.randint(seeds[5], (N_GX, N_GY), 0, 2), jax.random.fold_in(seeds[5], 1), 0, 1).astype(jnp.int32),
    }


ramp_rate = 0.7
decay_rate = 0.25
shade_scale = 0.1


def vertical(field):
    zero = jnp.zeros((1,) + field.shape[1:], jnp.float32)
    upper = jnp.concatenate([field[1:], zero], axis=0)
    lower = jnp.concatenate([zero, field[:-1]], axis=0)
    return upper - lower


def pad_xy(field):
    return jnp.pad(field, ((0, 0), (1, 1), (1, 1)))


def shading(terrain, shadow_len, sector, land_mask):
    ntile = NX // CX
    local = (jnp.arange(NX) % CX).astype(jnp.float32)
    ramp = (ramp_rate * local / CX)[:, None]
    west_terms = (jnp.exp(terrain + ramp) * (shade_scale / CX)).reshape(ntile, CX, NY)
    east_terms = (jnp.exp(terrain - ramp) * (shade_scale / CX)).reshape(ntile, CX, NY)
    prefix = jnp.cumsum(west_terms, axis=1) - west_terms
    suffix = jnp.sum(east_terms, axis=1, keepdims=True) - jnp.cumsum(east_terms, axis=1)
    west_tot = jnp.sum(west_terms, axis=1)
    east_tot = jnp.sum(east_terms, axis=1)
    tiles = jnp.arange(ntile)
    dist = (tiles[:, None] - tiles[None, :])[:, :, None]
    reach = shadow_len[None, None, :]
    west_wt = jnp.where((dist >= 1) & (dist <= reach), jnp.exp(-decay_rate * dist.astype(jnp.float32)), 0.0)
    east_wt = jnp.where((-dist >= 1) & (-dist <= reach), jnp.exp(decay_rate * dist.astype(jnp.float32)), 0.0)
    west_far = jnp.sum(west_wt * west_tot[None, :, :], axis=1)
    east_far = jnp.sum(east_wt * east_tot[None, :, :], axis=1)
    west_occ = ((prefix + west_far[:, None, :]).reshape(NX, NY)) * jnp.exp(-terrain - ramp)
    east_occ = ((suffix + east_far[:, None, :]).reshape(NX, NY)) * jnp.exp(ramp - terrain)
    sun = jnp.where(sector[None, :] == 0, 1.0 / (1.0 + west_occ), 1.0 / (1.0 + east_occ))
    sky = 1.0 / (1.0 + 0.5 * (west_occ + east_occ))
    land = jnp.repeat(jnp.repeat(land_mask, CX, axis=0), CY, axis=1).astype(jnp.float32)
    return land * (0.7 * sun + 0.3 * sky) + (1.0 - land) * 0.3 * sky


def reference(winds, thermo, terrain, shadow_len, sector, land_mask):
    heating = shading(terrain, shadow_len, sector, land_mask)
    profile = jnp.exp(-jnp.arange(K).astype(jnp.float32) / 4.0)
    heat_term = profile[:, None, None] * heating[None]
    east_v, north_v, up_v = winds[0], winds[1], winds[2]
    press, theta, moist = thermo[0], thermo[1], thermo[2]
    for step in range(ITERS):
        pp = pad_xy(press)
        tp = pad_xy(theta)
        qp = pad_xy(moist)
        east_n = east_v - 0.25 * (pp[:, 2:, 1:-1] - pp[:, :-2, 1:-1])
        north_n = north_v - 0.25 * (pp[:, 1:-1, 2:] - pp[:, 1:-1, :-2])
        up_n = up_v - 0.25 * vertical(press) + 0.1 * theta
        lap_t = tp[:, 2:, 1:-1] + tp[:, :-2, 1:-1] + tp[:, 1:-1, 2:] + tp[:, 1:-1, :-2] - 4.0 * theta
        theta_n = theta + 0.1 * lap_t - 0.15 * (tp[:, 2:, 1:-1] - tp[:, :-2, 1:-1]) - 0.1 * up_n + heat_term
        lap_q = qp[:, 2:, 1:-1] + qp[:, :-2, 1:-1] + qp[:, 1:-1, 2:] + qp[:, 1:-1, :-2] - 4.0 * moist
        moist_n = moist + 0.1 * lap_q - 0.15 * (qp[:, 2:, 1:-1] - qp[:, :-2, 1:-1])
        up_pad = pad_xy(east_n)
        vp_pad = pad_xy(north_n)
        diverge = (up_pad[:, 2:, 1:-1] - up_pad[:, :-2, 1:-1]) + (vp_pad[:, 1:-1, 2:] - vp_pad[:, 1:-1, :-2])
        press = press - 0.25 * (diverge + vertical(up_n))
        east_v, north_v, up_v, theta, moist = east_n, north_n, up_n, theta_n, moist_n
    return jnp.stack([east_v, north_v, up_v]), jnp.stack([press, theta, moist])
```

```python
import math

import jax
import jax.numpy as jnp
from jax import lax
from jax.sharding import PartitionSpec as P

ITERS = 2
LMAX = 4


ramp_rate = 0.7
decay_rate = 0.25
shade_scale = 0.1


def shifted(block, axis, distance):
    devices = range(lax.axis_size(axis))
    route = [(i, i + distance) for i in devices if i + distance in devices]
    return lax.ppermute(block, axis, route)


def vertical(field):
    zero = jnp.zeros((1,) + field.shape[1:], jnp.float32)
    upper = jnp.concatenate([field[1:], zero], axis=0)
    lower = jnp.concatenate([zero, field[:-1]], axis=0)
    return upper - lower


def edge_rows(p, across, fields, dim):
    n = p.shape[dim]
    take = lambda f, i: lax.index_in_dim(f, i, axis=dim, keepdims=False)
    high = [take(p, n - 2), take(p, n - 1), take(across, n - 1)] + [take(f, n - 1) for f in fields]
    low = [take(p, 1), take(p, 0), take(across, 0)] + [take(f, 0) for f in fields]
    return jnp.stack(high), jnp.stack(low)


def substep(state, halos, heat_term, first_x, last_x, first_y, last_y):
    east_v, north_v, up_v, press, theta, moist = state
    from_xm, from_xp, from_ym, from_yp = halos
    ex = lambda a: a[:, None, :]
    ey = lambda a: a[:, :, None]
    p_x = jnp.concatenate([ex(from_xm[0]), ex(from_xm[1]), press, ex(from_xp[1]), ex(from_xp[0])], axis=1)
    p_y = jnp.concatenate([ey(from_ym[0]), ey(from_ym[1]), press, ey(from_yp[1]), ey(from_yp[0])], axis=2)
    u_x = jnp.concatenate([ex(from_xm[2]), east_v, ex(from_xp[2])], axis=1)
    v_y = jnp.concatenate([ey(from_ym[2]), north_v, ey(from_yp[2])], axis=2)
    u1_x = u_x - 0.25 * (p_x[:, 2:] - p_x[:, :-2])
    v1_y = v_y - 0.25 * (p_y[:, :, 2:] - p_y[:, :, :-2])
    nx, ny = press.shape[1], press.shape[2]
    xi = lax.broadcasted_iota(jnp.int32, (1, nx + 2, 1), 1)
    yi = lax.broadcasted_iota(jnp.int32, (1, 1, ny + 2), 2)
    dead_x = ((xi == 0) & first_x) | ((xi == nx + 1) & last_x)
    dead_y = ((yi == 0) & first_y) | ((yi == ny + 1) & last_y)
    u1_x = jnp.where(dead_x, 0.0, u1_x)
    v1_y = jnp.where(dead_y, 0.0, v1_y)
    up_n = up_v - 0.25 * vertical(press) + 0.1 * theta
    results = []
    for index, field in ((3, theta), (4, moist)):
        f_x = jnp.concatenate([ex(from_xm[index]), field, ex(from_xp[index])], axis=1)
        f_y = jnp.concatenate([ey(from_ym[index]), field, ey(from_yp[index])], axis=2)
        east_c = f_x[:, 2:]
        west_c = f_x[:, :-2]
        lap = east_c + west_c + f_y[:, :, 2:] + f_y[:, :, :-2] - 4.0 * field
        results.append(field + 0.1 * lap - 0.15 * (east_c - west_c))
    theta_n = results[0] - 0.1 * up_n + heat_term
    moist_n = results[1]
    diverge = (u1_x[:, 2:] - u1_x[:, :-2]) + (v1_y[:, :, 2:] - v1_y[:, :, :-2])
    press_n = press - 0.25 * (diverge + vertical(up_n))
    east_n = u1_x[:, 1:-1]
    north_n = v1_y[:, :, 1:-1]
    return (east_n, north_n, up_n, press_n, theta_n, moist_n)


def per_device(winds, thermo, terrain, shadow_len, sector, land_mask):
    cols_x, cols_y = terrain.shape
    levels = winds.shape[1]
    nxd = lax.axis_size("gx")
    nyd = lax.axis_size("gy")
    ix = lax.axis_index("gx")
    iy = lax.axis_index("gy")
    first_x, last_x = ix == 0, ix == nxd - 1
    first_y, last_y = iy == 0, iy == nyd - 1
    ramp = (ramp_rate * jnp.arange(cols_x).astype(jnp.float32) / cols_x)[:, None]
    west_terms = jnp.exp(terrain + ramp) * (shade_scale / cols_x)
    east_terms = jnp.exp(terrain - ramp) * (shade_scale / cols_x)
    prefix = jnp.cumsum(west_terms, axis=0) - west_terms
    west_tot = jnp.sum(west_terms, axis=0)
    east_tot = jnp.sum(east_terms, axis=0)
    suffix = east_tot[None, :] - jnp.cumsum(east_terms, axis=0)

    state = (winds[0], winds[1], winds[2], thermo[0], thermo[1], thermo[2])
    halos = None
    far = {}
    for step in range(ITERS):
        east_v, north_v, up_v, press, theta, moist = state
        to_xp, to_xm = edge_rows(press, east_v, (theta, moist), 1)
        to_yp, to_ym = edge_rows(press, north_v, (theta, moist), 2)
        if step == 0:
            to_xp = jnp.concatenate([to_xp.reshape(-1, cols_y), west_tot[None]], axis=0)
            to_xm = jnp.concatenate([to_xm.reshape(-1, cols_y), east_tot[None]], axis=0)
        from_xm = shifted(to_xp, "gx", 1)
        from_xp = shifted(to_xm, "gx", -1)
        from_ym = shifted(to_yp, "gy", 1)
        from_yp = shifted(to_ym, "gy", -1)
        if step == 0:
            for reach in range(2, LMAX + 1):
                far[("w", reach)] = shifted(west_tot, "gx", reach)
                far[("e", reach)] = shifted(east_tot, "gx", -reach)
            far[("w", 1)] = from_xm[-1]
            far[("e", 1)] = from_xp[-1]
            from_xm = from_xm[:-1].reshape(5, levels, cols_y)
            from_xp = from_xp[:-1].reshape(5, levels, cols_y)
            west_far = jnp.zeros((cols_y,), jnp.float32)
            east_far = jnp.zeros((cols_y,), jnp.float32)
            for reach in range(1, LMAX + 1):
                weight = jnp.where(shadow_len >= reach, math.exp(-decay_rate * reach), 0.0)
                west_far = west_far + weight * far[("w", reach)]
                east_far = east_far + weight * far[("e", reach)]
            west_occ = (prefix + west_far[None, :]) * jnp.exp(-terrain - ramp)
            east_occ = (suffix + east_far[None, :]) * jnp.exp(ramp - terrain)
            sun = jnp.where(sector[None, :] == 0, 1.0 / (1.0 + west_occ), 1.0 / (1.0 + east_occ))
            sky = 1.0 / (1.0 + 0.5 * (west_occ + east_occ))
            land = land_mask[0, 0].astype(jnp.float32)
            heating = land * (0.7 * sun + 0.3 * sky) + (1.0 - land) * 0.3 * sky
            profile = jnp.exp(-jnp.arange(levels).astype(jnp.float32) / 4.0)
            heat_term = profile[:, None, None] * heating[None]
        halos = (from_xm, from_xp, from_ym, from_yp)
        state = substep(state, halos, heat_term, first_x, last_x, first_y, last_y)
    east_v, north_v, up_v, press, theta, moist = state
    return (jnp.stack([east_v, north_v, up_v]), jnp.stack([press, theta, moist]))


def solution(mesh):
    return jax.shard_map(
        per_device,
        mesh=mesh,
        in_specs=(
            P(None, None, "gx", "gy"),
            P(None, None, "gx", "gy"),
            P("gx", "gy"),
            P("gy"),
            P("gy"),
            P("gx", "gy"),
        ),
        out_specs=(P(None, None, "gx", "gy"), P(None, None, "gx", "gy")),
        check_vma=False,
    )
```

```python
import math

import jax
import jax.numpy as jnp
from jax import lax
from jax.sharding import PartitionSpec as P

ITERS = 2
LMAX = 4


ramp_rate = 0.7
decay_rate = 0.25
shade_scale = 0.1


def shifted(block, axis, distance):
    devices = range(lax.axis_size(axis))
    route = [(i, i + distance) for i in devices if i + distance in devices]
    return lax.ppermute(block, axis, route)


def vertical(field):
    zero = jnp.zeros((1,) + field.shape[1:], jnp.float32)
    upper = jnp.concatenate([field[1:], zero], axis=0)
    lower = jnp.concatenate([zero, field[:-1]], axis=0)
    return upper - lower


def edge_rows(p, across, fields, dim):
    n = p.shape[dim]
    take = lambda f, i: lax.index_in_dim(f, i, axis=dim, keepdims=False)
    high = [take(p, n - 2), take(p, n - 1), take(across, n - 1)] + [take(f, n - 1) for f in fields]
    low = [take(p, 1), take(p, 0), take(across, 0)] + [take(f, 0) for f in fields]
    return jnp.stack(high), jnp.stack(low)


def substep(state, halos, heat_term, first_x, last_x, first_y, last_y):
    east_v, north_v, up_v, press, theta, moist = state
    from_xm, from_xp, from_ym, from_yp = halos
    ex = lambda a: a[:, None, :]
    ey = lambda a: a[:, :, None]
    p_x = jnp.concatenate([ex(from_xm[0]), ex(from_xm[1]), press, ex(from_xp[1]), ex(from_xp[0])], axis=1)
    p_y = jnp.concatenate([ey(from_ym[0]), ey(from_ym[1]), press, ey(from_yp[1]), ey(from_yp[0])], axis=2)
    u_x = jnp.concatenate([ex(from_xm[2]), east_v, ex(from_xp[2])], axis=1)
    v_y = jnp.concatenate([ey(from_ym[2]), north_v, ey(from_yp[2])], axis=2)
    u1_x = u_x - 0.25 * (p_x[:, 2:] - p_x[:, :-2])
    v1_y = v_y - 0.25 * (p_y[:, :, 2:] - p_y[:, :, :-2])
    nx, ny = press.shape[1], press.shape[2]
    xi = lax.broadcasted_iota(jnp.int32, (1, nx + 2, 1), 1)
    yi = lax.broadcasted_iota(jnp.int32, (1, 1, ny + 2), 2)
    dead_x = ((xi == 0) & first_x) | ((xi == nx + 1) & last_x)
    dead_y = ((yi == 0) & first_y) | ((yi == ny + 1) & last_y)
    u1_x = jnp.where(dead_x, 0.0, u1_x)
    v1_y = jnp.where(dead_y, 0.0, v1_y)
    up_n = up_v - 0.25 * vertical(press) + 0.1 * theta
    results = []
    for index, field in ((3, theta), (4, moist)):
        f_x = jnp.concatenate([ex(from_xm[index]), field, ex(from_xp[index])], axis=1)
        f_y = jnp.concatenate([ey(from_ym[index]), field, ey(from_yp[index])], axis=2)
        east_c = f_x[:, 2:]
        west_c = f_x[:, :-2]
        lap = east_c + west_c + f_y[:, :, 2:] + f_y[:, :, :-2] - 4.0 * field
        results.append(field + 0.1 * lap - 0.15 * (east_c - west_c))
    theta_n = results[0] - 0.1 * up_n + heat_term
    moist_n = results[1]
    diverge = (u1_x[:, 2:] - u1_x[:, :-2]) + (v1_y[:, :, 2:] - v1_y[:, :, :-2])
    press_n = press - 0.25 * (diverge + vertical(up_n))
    east_n = u1_x[:, 1:-1]
    north_n = v1_y[:, :, 1:-1]
    return (east_n, north_n, up_n, press_n, theta_n, moist_n)


def per_device(winds, thermo, terrain, shadow_len, sector, land_mask):
    cols_x, cols_y = terrain.shape
    levels = winds.shape[1]
    nxd = lax.axis_size("gx")
    nyd = lax.axis_size("gy")
    ix = lax.axis_index("gx")
    iy = lax.axis_index("gy")
    first_x, last_x = ix == 0, ix == nxd - 1
    first_y, last_y = iy == 0, iy == nyd - 1
    ramp = (ramp_rate * jnp.arange(cols_x).astype(jnp.float32) / cols_x)[:, None]
    west_terms = jnp.exp(terrain + ramp) * (shade_scale / cols_x)
    east_terms = jnp.exp(terrain - ramp) * (shade_scale / cols_x)
    prefix = jnp.cumsum(west_terms, axis=0) - west_terms
    west_tot = jnp.sum(west_terms, axis=0)
    east_tot = jnp.sum(east_terms, axis=0)
    suffix = east_tot[None, :] - jnp.cumsum(east_terms, axis=0)

    state = (winds[0], winds[1], winds[2], thermo[0], thermo[1], thermo[2])
    halos = None
    for step in range(ITERS):
        east_v, north_v, up_v, press, theta, moist = state
        to_xp, to_xm = edge_rows(press, east_v, (theta, moist), 1)
        to_yp, to_ym = edge_rows(press, north_v, (theta, moist), 2)
        from_xm = shifted(to_xp, "gx", 1)
        from_xp = shifted(to_xm, "gx", -1)
        from_ym = shifted(to_yp, "gy", 1)
        from_yp = shifted(to_ym, "gy", -1)
        if step == 0:
            tots = lax.all_gather(jnp.stack([west_tot, east_tot]), "gx")
            pad = jnp.zeros((LMAX,) + tots.shape[1:], jnp.float32)
            near = lax.dynamic_slice_in_dim(jnp.concatenate([pad, tots, pad]), ix, 2 * LMAX + 1)
            west_far = jnp.zeros((cols_y,), jnp.float32)
            east_far = jnp.zeros((cols_y,), jnp.float32)
            for reach in range(1, LMAX + 1):
                weight = jnp.where(shadow_len >= reach, math.exp(-decay_rate * reach), 0.0)
                west_far = west_far + weight * near[LMAX - reach, 0]
                east_far = east_far + weight * near[LMAX + reach, 1]
            west_occ = (prefix + west_far[None, :]) * jnp.exp(-terrain - ramp)
            east_occ = (suffix + east_far[None, :]) * jnp.exp(ramp - terrain)
            sun = jnp.where(sector[None, :] == 0, 1.0 / (1.0 + west_occ), 1.0 / (1.0 + east_occ))
            sky = 1.0 / (1.0 + 0.5 * (west_occ + east_occ))
            land = land_mask[0, 0].astype(jnp.float32)
            heating = land * (0.7 * sun + 0.3 * sky) + (1.0 - land) * 0.3 * sky
            profile = jnp.exp(-jnp.arange(levels).astype(jnp.float32) / 4.0)
            heat_term = profile[:, None, None] * heating[None]
        halos = (from_xm, from_xp, from_ym, from_yp)
        state = substep(state, halos, heat_term, first_x, last_x, first_y, last_y)
    east_v, north_v, up_v, press, theta, moist = state
    return (jnp.stack([east_v, north_v, up_v]), jnp.stack([press, theta, moist]))


def solution(mesh):
    return jax.shard_map(
        per_device,
        mesh=mesh,
        in_specs=(
            P(None, None, "gx", "gy"),
            P(None, None, "gx", "gy"),
            P("gx", "gy"),
            P("gy"),
            P("gy"),
            P("gx", "gy"),
        ),
        out_specs=(P(None, None, "gx", "gy"), P(None, None, "gx", "gy")),
        check_vma=False,
    )
```

```python
import math

import jax
import jax.numpy as jnp
from jax import lax
from jax.sharding import PartitionSpec as P

ITERS = 2
LMAX = 4


ramp_rate = 0.7
decay_rate = 0.25
shade_scale = 0.1


def shifted(block, axis, distance):
    devices = range(lax.axis_size(axis))
    route = [(i, i + distance) for i in devices if i + distance in devices]
    return lax.ppermute(block, axis, route)


def vertical(field):
    zero = jnp.zeros((1,) + field.shape[1:], jnp.float32)
    upper = jnp.concatenate([field[1:], zero], axis=0)
    lower = jnp.concatenate([zero, field[:-1]], axis=0)
    return upper - lower


def edge_rows(p, across, fields, dim):
    n = p.shape[dim]
    take = lambda f, i: lax.index_in_dim(f, i, axis=dim, keepdims=False)
    high = [take(p, n - 2), take(p, n - 1), take(across, n - 1)] + [take(f, n - 1) for f in fields]
    low = [take(p, 1), take(p, 0), take(across, 0)] + [take(f, 0) for f in fields]
    return jnp.stack(high), jnp.stack(low)


def substep(state, halos, heat_term, first_x, last_x, first_y, last_y):
    east_v, north_v, up_v, press, theta, moist = state
    from_xm, from_xp, from_ym, from_yp = halos
    ex = lambda a: a[:, None, :]
    ey = lambda a: a[:, :, None]
    p_x = jnp.concatenate([ex(from_xm[0]), ex(from_xm[1]), press, ex(from_xp[1]), ex(from_xp[0])], axis=1)
    p_y = jnp.concatenate([ey(from_ym[0]), ey(from_ym[1]), press, ey(from_yp[1]), ey(from_yp[0])], axis=2)
    u_x = jnp.concatenate([ex(from_xm[2]), east_v, ex(from_xp[2])], axis=1)
    v_y = jnp.concatenate([ey(from_ym[2]), north_v, ey(from_yp[2])], axis=2)
    u1_x = u_x - 0.25 * (p_x[:, 2:] - p_x[:, :-2])
    v1_y = v_y - 0.25 * (p_y[:, :, 2:] - p_y[:, :, :-2])
    nx, ny = press.shape[1], press.shape[2]
    xi = lax.broadcasted_iota(jnp.int32, (1, nx + 2, 1), 1)
    yi = lax.broadcasted_iota(jnp.int32, (1, 1, ny + 2), 2)
    dead_x = ((xi == 0) & first_x) | ((xi == nx + 1) & last_x)
    dead_y = ((yi == 0) & first_y) | ((yi == ny + 1) & last_y)
    u1_x = jnp.where(dead_x, 0.0, u1_x)
    v1_y = jnp.where(dead_y, 0.0, v1_y)
    up_n = up_v - 0.25 * vertical(press) + 0.1 * theta
    results = []
    for index, field in ((3, theta), (4, moist)):
        f_x = jnp.concatenate([ex(from_xm[index]), field, ex(from_xp[index])], axis=1)
        f_y = jnp.concatenate([ey(from_ym[index]), field, ey(from_yp[index])], axis=2)
        east_c = f_x[:, 2:]
        west_c = f_x[:, :-2]
        lap = east_c + west_c + f_y[:, :, 2:] + f_y[:, :, :-2] - 4.0 * field
        results.append(field + 0.1 * lap - 0.15 * (east_c - west_c))
    theta_n = results[0] - 0.1 * up_n + heat_term
    moist_n = results[1]
    diverge = (u1_x[:, 2:] - u1_x[:, :-2]) + (v1_y[:, :, 2:] - v1_y[:, :, :-2])
    press_n = press - 0.25 * (diverge + vertical(up_n))
    east_n = u1_x[:, 1:-1]
    north_n = v1_y[:, :, 1:-1]
    return (east_n, north_n, up_n, press_n, theta_n, moist_n)


def per_device(winds, thermo, terrain, shadow_len, sector, land_mask):
    cols_x, cols_y = terrain.shape
    levels = winds.shape[1]
    nxd = lax.axis_size("gx")
    nyd = lax.axis_size("gy")
    ix = lax.axis_index("gx")
    iy = lax.axis_index("gy")
    first_x, last_x = ix == 0, ix == nxd - 1
    first_y, last_y = iy == 0, iy == nyd - 1
    ramp = (ramp_rate * jnp.arange(cols_x).astype(jnp.float32) / cols_x)[:, None]
    west_terms = jnp.exp(terrain + ramp) * (shade_scale / cols_x)
    east_terms = jnp.exp(terrain - ramp) * (shade_scale / cols_x)
    prefix = jnp.cumsum(west_terms, axis=0) - west_terms
    west_tot = jnp.sum(west_terms, axis=0)
    east_tot = jnp.sum(east_terms, axis=0)
    suffix = east_tot[None, :] - jnp.cumsum(east_terms, axis=0)

    state = (winds[0], winds[1], winds[2], thermo[0], thermo[1], thermo[2])
    halos = None
    far = {}
    for step in range(ITERS):
        east_v, north_v, up_v, press, theta, moist = state
        to_xp, to_xm = edge_rows(press, east_v, (theta, moist), 1)
        to_yp, to_ym = edge_rows(press, north_v, (theta, moist), 2)
        if step == 0:
            to_xp = jnp.concatenate([to_xp.reshape(-1, cols_y), west_tot[None]], axis=0)
            to_xm = jnp.concatenate([to_xm.reshape(-1, cols_y), east_tot[None]], axis=0)
        from_xm = shifted(to_xp, "gx", 1)
        from_xp = shifted(to_xm, "gx", -1)
        from_ym = shifted(to_yp, "gy", 1)
        from_yp = shifted(to_ym, "gy", -1)
        if step == 0:
            near_w = shifted(west_tot, "gx", 2)
            near_e = shifted(east_tot, "gx", -2)
            far[("w", 1)] = from_xm[-1]
            far[("e", 1)] = from_xp[-1]
            far[("w", 2)] = near_w
            far[("e", 2)] = near_e
            relay_w = shifted(jnp.stack([far[("w", 1)], near_w]), "gx", 2)
            relay_e = shifted(jnp.stack([far[("e", 1)], near_e]), "gx", -2)
            far[("w", 3)], far[("w", 4)] = relay_w[0], relay_w[1]
            far[("e", 3)], far[("e", 4)] = relay_e[0], relay_e[1]
            from_xm = from_xm[:-1].reshape(5, levels, cols_y)
            from_xp = from_xp[:-1].reshape(5, levels, cols_y)
            west_far = jnp.zeros((cols_y,), jnp.float32)
            east_far = jnp.zeros((cols_y,), jnp.float32)
            for reach in range(1, LMAX + 1):
                weight = jnp.where(shadow_len >= reach, math.exp(-decay_rate * reach), 0.0)
                west_far = west_far + weight * far[("w", reach)]
                east_far = east_far + weight * far[("e", reach)]
            west_occ = (prefix + west_far[None, :]) * jnp.exp(-terrain - ramp)
            east_occ = (suffix + east_far[None, :]) * jnp.exp(ramp - terrain)
            sun = jnp.where(sector[None, :] == 0, 1.0 / (1.0 + west_occ), 1.0 / (1.0 + east_occ))
            sky = 1.0 / (1.0 + 0.5 * (west_occ + east_occ))
            land = land_mask[0, 0].astype(jnp.float32)
            heating = land * (0.7 * sun + 0.3 * sky) + (1.0 - land) * 0.3 * sky
            profile = jnp.exp(-jnp.arange(levels).astype(jnp.float32) / 4.0)
            heat_term = profile[:, None, None] * heating[None]
        halos = (from_xm, from_xp, from_ym, from_yp)
        state = substep(state, halos, heat_term, first_x, last_x, first_y, last_y)
    east_v, north_v, up_v, press, theta, moist = state
    return (jnp.stack([east_v, north_v, up_v]), jnp.stack([press, theta, moist]))


def solution(mesh):
    return jax.shard_map(
        per_device,
        mesh=mesh,
        in_specs=(
            P(None, None, "gx", "gy"),
            P(None, None, "gx", "gy"),
            P("gx", "gy"),
            P("gy"),
            P("gy"),
            P("gx", "gy"),
        ),
        out_specs=(P(None, None, "gx", "gy"), P(None, None, "gx", "gy")),
        check_vma=False,
    )
```

```python
import math

import jax
import jax.numpy as jnp
from jax import lax
from jax.sharding import PartitionSpec as P

ITERS = 2
LMAX = 4


ramp_rate = 0.7
decay_rate = 0.25
shade_scale = 0.1


def shifted(block, axis, distance):
    devices = range(lax.axis_size(axis))
    route = [(i, i + distance) for i in devices if i + distance in devices]
    return lax.ppermute(block, axis, route)


def vertical(field):
    zero = jnp.zeros((1,) + field.shape[1:], jnp.float32)
    upper = jnp.concatenate([field[1:], zero], axis=0)
    lower = jnp.concatenate([zero, field[:-1]], axis=0)
    return upper - lower


def edge_rows(p, across, fields, dim):
    n = p.shape[dim]
    take = lambda f, i: lax.index_in_dim(f, i, axis=dim, keepdims=False)
    high = [take(p, n - 2), take(p, n - 1), take(across, n - 1)] + [take(f, n - 1) for f in fields]
    low = [take(p, 1), take(p, 0), take(across, 0)] + [take(f, 0) for f in fields]
    return jnp.stack(high), jnp.stack(low)


def substep(state, halos, heat_term, first_x, last_x, first_y, last_y):
    east_v, north_v, up_v, press, theta, moist = state
    from_xm, from_xp, from_ym, from_yp = halos
    ex = lambda a: a[:, None, :]
    ey = lambda a: a[:, :, None]
    p_x = jnp.concatenate([ex(from_xm[0]), ex(from_xm[1]), press, ex(from_xp[1]), ex(from_xp[0])], axis=1)
    p_y = jnp.concatenate([ey(from_ym[0]), ey(from_ym[1]), press, ey(from_yp[1]), ey(from_yp[0])], axis=2)
    u_x = jnp.concatenate([ex(from_xm[2]), east_v, ex(from_xp[2])], axis=1)
    v_y = jnp.concatenate([ey(from_ym[2]), north_v, ey(from_yp[2])], axis=2)
    u1_x = u_x - 0.25 * (p_x[:, 2:] - p_x[:, :-2])
    v1_y = v_y - 0.25 * (p_y[:, :, 2:] - p_y[:, :, :-2])
    nx, ny = press.shape[1], press.shape[2]
    xi = lax.broadcasted_iota(jnp.int32, (1, nx + 2, 1), 1)
    yi = lax.broadcasted_iota(jnp.int32, (1, 1, ny + 2), 2)
    dead_x = ((xi == 0) & first_x) | ((xi == nx + 1) & last_x)
    dead_y = ((yi == 0) & first_y) | ((yi == ny + 1) & last_y)
    u1_x = jnp.where(dead_x, 0.0, u1_x)
    v1_y = jnp.where(dead_y, 0.0, v1_y)
    up_n = up_v - 0.25 * vertical(press) + 0.1 * theta
    results = []
    for index, field in ((3, theta), (4, moist)):
        f_x = jnp.concatenate([ex(from_xm[index]), field, ex(from_xp[index])], axis=1)
        f_y = jnp.concatenate([ey(from_ym[index]), field, ey(from_yp[index])], axis=2)
        east_c = f_x[:, 2:]
        west_c = f_x[:, :-2]
        lap = east_c + west_c + f_y[:, :, 2:] + f_y[:, :, :-2] - 4.0 * field
        results.append(field + 0.1 * lap - 0.15 * (east_c - west_c))
    theta_n = results[0] - 0.1 * up_n + heat_term
    moist_n = results[1]
    diverge = (u1_x[:, 2:] - u1_x[:, :-2]) + (v1_y[:, :, 2:] - v1_y[:, :, :-2])
    press_n = press - 0.25 * (diverge + vertical(up_n))
    east_n = u1_x[:, 1:-1]
    north_n = v1_y[:, :, 1:-1]
    return (east_n, north_n, up_n, press_n, theta_n, moist_n)


def per_device(winds, thermo, terrain, shadow_len, sector, land_mask):
    cols_x, cols_y = terrain.shape
    levels = winds.shape[1]
    nxd = lax.axis_size("gx")
    nyd = lax.axis_size("gy")
    ix = lax.axis_index("gx")
    iy = lax.axis_index("gy")
    first_x, last_x = ix == 0, ix == nxd - 1
    first_y, last_y = iy == 0, iy == nyd - 1
    ramp = (ramp_rate * jnp.arange(cols_x).astype(jnp.float32) / cols_x)[:, None]
    west_terms = jnp.exp(terrain + ramp) * (shade_scale / cols_x)
    east_terms = jnp.exp(terrain - ramp) * (shade_scale / cols_x)
    prefix = jnp.cumsum(west_terms, axis=0) - west_terms
    west_tot = jnp.sum(west_terms, axis=0)
    east_tot = jnp.sum(east_terms, axis=0)
    suffix = east_tot[None, :] - jnp.cumsum(east_terms, axis=0)

    state = (winds[0], winds[1], winds[2], thermo[0], thermo[1], thermo[2])
    halos = None
    far = {}
    for step in range(ITERS):
        east_v, north_v, up_v, press, theta, moist = state
        to_xp, to_xm = edge_rows(press, east_v, (theta, moist), 1)
        to_yp, to_ym = edge_rows(press, north_v, (theta, moist), 2)
        if step == 0:
            to_xp = jnp.concatenate([to_xp.reshape(-1, cols_y), west_tot[None]], axis=0)
            to_xm = jnp.concatenate([to_xm.reshape(-1, cols_y), east_tot[None]], axis=0)
        from_xm = shifted(to_xp, "gx", 1)
        from_xp = shifted(to_xm, "gx", -1)
        from_ym = shifted(to_yp, "gy", 1)
        from_yp = shifted(to_ym, "gy", -1)
        if step == 0:
            near_w = shifted(west_tot, "gx", 2)
            far[("w", 1)] = from_xm[-1]
            far[("e", 1)] = from_xp[-1]
            far[("w", 2)] = near_w
            relay_w = shifted(jnp.stack([far[("w", 1)], near_w]), "gx", 2)
            relay_e = shifted(jnp.stack([east_tot, far[("e", 1)]]), "gx", -2)
            far[("e", 4)] = shifted(far[("e", 1)], "gx", -3)
            far[("w", 3)], far[("w", 4)] = relay_w[0], relay_w[1]
            far[("e", 2)], far[("e", 3)] = relay_e[0], relay_e[1]
            from_xm = from_xm[:-1].reshape(5, levels, cols_y)
            from_xp = from_xp[:-1].reshape(5, levels, cols_y)
            west_far = jnp.zeros((cols_y,), jnp.float32)
            east_far = jnp.zeros((cols_y,), jnp.float32)
            for reach in range(1, LMAX + 1):
                weight = jnp.where(shadow_len >= reach, math.exp(-decay_rate * reach), 0.0)
                west_far = west_far + weight * far[("w", reach)]
                east_far = east_far + weight * far[("e", reach)]
            west_occ = (prefix + west_far[None, :]) * jnp.exp(-terrain - ramp)
            east_occ = (suffix + east_far[None, :]) * jnp.exp(ramp - terrain)
            sun = jnp.where(sector[None, :] == 0, 1.0 / (1.0 + west_occ), 1.0 / (1.0 + east_occ))
            sky = 1.0 / (1.0 + 0.5 * (west_occ + east_occ))
            land = land_mask[0, 0].astype(jnp.float32)
            heating = land * (0.7 * sun + 0.3 * sky) + (1.0 - land) * 0.3 * sky
            profile = jnp.exp(-jnp.arange(levels).astype(jnp.float32) / 4.0)
            heat_term = profile[:, None, None] * heating[None]
        halos = (from_xm, from_xp, from_ym, from_yp)
        state = substep(state, halos, heat_term, first_x, last_x, first_y, last_y)
    east_v, north_v, up_v, press, theta, moist = state
    return (jnp.stack([east_v, north_v, up_v]), jnp.stack([press, theta, moist]))


def solution(mesh):
    return jax.shard_map(
        per_device,
        mesh=mesh,
        in_specs=(
            P(None, None, "gx", "gy"),
            P(None, None, "gx", "gy"),
            P("gx", "gy"),
            P("gy"),
            P("gy"),
            P("gx", "gy"),
        ),
        out_specs=(P(None, None, "gx", "gy"), P(None, None, "gx", "gy")),
        check_vma=False,
    )
```

```python
import math

import jax
import jax.numpy as jnp
from jax import lax
from jax.sharding import PartitionSpec as P

ITERS = 2
LMAX = 4


ramp_rate = 0.7
decay_rate = 0.25
shade_scale = 0.1


def shifted(block, axis, distance):
    devices = range(lax.axis_size(axis))
    route = [(i, i + distance) for i in devices if i + distance in devices]
    return lax.ppermute(block, axis, route)


def vertical(field):
    zero = jnp.zeros((1,) + field.shape[1:], jnp.float32)
    upper = jnp.concatenate([field[1:], zero], axis=0)
    lower = jnp.concatenate([zero, field[:-1]], axis=0)
    return upper - lower


def edge_rows(p, across, fields, dim):
    n = p.shape[dim]
    take = lambda f, i: lax.index_in_dim(f, i, axis=dim, keepdims=False)
    high = [take(p, n - 2), take(p, n - 1), take(across, n - 1)] + [take(f, n - 1) for f in fields]
    low = [take(p, 1), take(p, 0), take(across, 0)] + [take(f, 0) for f in fields]
    return jnp.stack(high), jnp.stack(low)


def substep(state, halos, heat_term, first_x, last_x, first_y, last_y):
    east_v, north_v, up_v, press, theta, moist = state
    from_xm, from_xp, from_ym, from_yp = halos
    nx, ny = press.shape[1], press.shape[2]
    row = lax.broadcasted_iota(jnp.int32, (1, nx, 1), 1)
    lane = lax.broadcasted_iota(jnp.int32, (1, 1, ny), 2)
    x_up = lambda f, h: jnp.where(row == nx - 1, h[:, None, :], jnp.roll(f, -1, axis=1))
    x_dn = lambda f, h: jnp.where(row == 0, h[:, None, :], jnp.roll(f, 1, axis=1))
    y_up = lambda f, h: jnp.where(lane == ny - 1, h[:, :, None], jnp.roll(f, -1, axis=2))
    y_dn = lambda f, h: jnp.where(lane == 0, h[:, :, None], jnp.roll(f, 1, axis=2))
    east_n = east_v - 0.25 * (x_up(press, from_xp[1]) - x_dn(press, from_xm[1]))
    north_n = north_v - 0.25 * (y_up(press, from_yp[1]) - y_dn(press, from_ym[1]))
    east_hi = from_xp[2] - 0.25 * (from_xp[0] - press[:, nx - 1, :])
    east_lo = from_xm[2] - 0.25 * (press[:, 0, :] - from_xm[0])
    north_hi = from_yp[2] - 0.25 * (from_yp[0] - press[:, :, ny - 1])
    north_lo = from_ym[2] - 0.25 * (press[:, :, 0] - from_ym[0])
    east_hi = jnp.where(last_x, 0.0, east_hi)
    east_lo = jnp.where(first_x, 0.0, east_lo)
    north_hi = jnp.where(last_y, 0.0, north_hi)
    north_lo = jnp.where(first_y, 0.0, north_lo)
    up_n = up_v - 0.25 * vertical(press) + 0.1 * theta
    results = []
    for index, field in ((3, theta), (4, moist)):
        east_c = x_up(field, from_xp[index])
        west_c = x_dn(field, from_xm[index])
        lap = east_c + west_c + y_up(field, from_yp[index]) + y_dn(field, from_ym[index]) - 4.0 * field
        results.append(field + 0.1 * lap - 0.15 * (east_c - west_c))
    theta_n = results[0] - 0.1 * up_n + heat_term
    moist_n = results[1]
    diverge = (x_up(east_n, east_hi) - x_dn(east_n, east_lo)) + (
        y_up(north_n, north_hi) - y_dn(north_n, north_lo)
    )
    press_n = press - 0.25 * (diverge + vertical(up_n))
    return (east_n, north_n, up_n, press_n, theta_n, moist_n)


def per_device(winds, thermo, terrain, shadow_len, sector, land_mask):
    cols_x, cols_y = terrain.shape
    levels = winds.shape[1]
    nxd = lax.axis_size("gx")
    nyd = lax.axis_size("gy")
    ix = lax.axis_index("gx")
    iy = lax.axis_index("gy")
    first_x, last_x = ix == 0, ix == nxd - 1
    first_y, last_y = iy == 0, iy == nyd - 1
    ramp = (ramp_rate * jnp.arange(cols_x).astype(jnp.float32) / cols_x)[:, None]
    west_terms = jnp.exp(terrain + ramp) * (shade_scale / cols_x)
    east_terms = jnp.exp(terrain - ramp) * (shade_scale / cols_x)
    prefix = jnp.cumsum(west_terms, axis=0) - west_terms
    west_tot = jnp.sum(west_terms, axis=0)
    east_tot = jnp.sum(east_terms, axis=0)
    suffix = east_tot[None, :] - jnp.cumsum(east_terms, axis=0)

    state = (winds[0], winds[1], winds[2], thermo[0], thermo[1], thermo[2])
    halos = None
    far = {}
    for step in range(ITERS):
        east_v, north_v, up_v, press, theta, moist = state
        to_xp, to_xm = edge_rows(press, east_v, (theta, moist), 1)
        to_yp, to_ym = edge_rows(press, north_v, (theta, moist), 2)
        if step == 0:
            to_xp = jnp.concatenate([to_xp.reshape(-1, cols_y), west_tot[None]], axis=0)
            to_xm = jnp.concatenate([to_xm.reshape(-1, cols_y), east_tot[None]], axis=0)
        from_xm = shifted(to_xp, "gx", 1)
        from_xp = shifted(to_xm, "gx", -1)
        from_ym = shifted(to_yp, "gy", 1)
        from_yp = shifted(to_ym, "gy", -1)
        if step == 0:
            near_w = shifted(west_tot, "gx", 2)
            near_e = shifted(east_tot, "gx", -2)
            far[("w", 1)] = from_xm[-1]
            far[("e", 1)] = from_xp[-1]
            far[("w", 2)] = near_w
            far[("e", 2)] = near_e
            relay_w = shifted(jnp.stack([far[("w", 1)], near_w]), "gx", 2)
            relay_e = shifted(jnp.stack([far[("e", 1)], near_e]), "gx", -2)
            far[("w", 3)], far[("w", 4)] = relay_w[0], relay_w[1]
            far[("e", 3)], far[("e", 4)] = relay_e[0], relay_e[1]
            from_xm = from_xm[:-1].reshape(5, levels, cols_y)
            from_xp = from_xp[:-1].reshape(5, levels, cols_y)
            west_far = jnp.zeros((cols_y,), jnp.float32)
            east_far = jnp.zeros((cols_y,), jnp.float32)
            for reach in range(1, LMAX + 1):
                weight = jnp.where(shadow_len >= reach, math.exp(-decay_rate * reach), 0.0)
                west_far = west_far + weight * far[("w", reach)]
                east_far = east_far + weight * far[("e", reach)]
            west_occ = (prefix + west_far[None, :]) * jnp.exp(-terrain - ramp)
            east_occ = (suffix + east_far[None, :]) * jnp.exp(ramp - terrain)
            sun = jnp.where(sector[None, :] == 0, 1.0 / (1.0 + west_occ), 1.0 / (1.0 + east_occ))
            sky = 1.0 / (1.0 + 0.5 * (west_occ + east_occ))
            land = land_mask[0, 0].astype(jnp.float32)
            heating = land * (0.7 * sun + 0.3 * sky) + (1.0 - land) * 0.3 * sky
            profile = jnp.exp(-jnp.arange(levels).astype(jnp.float32) / 4.0)
            heat_term = profile[:, None, None] * heating[None]
        halos = (from_xm, from_xp, from_ym, from_yp)
        state = substep(state, halos, heat_term, first_x, last_x, first_y, last_y)
    east_v, north_v, up_v, press, theta, moist = state
    return (jnp.stack([east_v, north_v, up_v]), jnp.stack([press, theta, moist]))


def solution(mesh):
    return jax.shard_map(
        per_device,
        mesh=mesh,
        in_specs=(
            P(None, None, "gx", "gy"),
            P(None, None, "gx", "gy"),
            P("gx", "gy"),
            P("gy"),
            P("gy"),
            P("gx", "gy"),
        ),
        out_specs=(P(None, None, "gx", "gy"), P(None, None, "gx", "gy")),
        check_vma=False,
    )
```

```python
import math

import jax
import jax.numpy as jnp
from jax import lax
from jax.experimental import pallas as pl
from jax.experimental.pallas import tpu as pltpu
from jax.sharding import PartitionSpec as P

ITERS = 2
LMAX = 4


ramp_rate = 0.7
decay_rate = 0.25
shade_scale = 0.1


def shifted(block, axis, distance):
    devices = range(lax.axis_size(axis))
    route = [(i, i + distance) for i in devices if i + distance in devices]
    return lax.ppermute(block, axis, route)


def vertical(field):
    zero = jnp.zeros((1,) + field.shape[1:], jnp.float32)
    upper = jnp.concatenate([field[1:], zero], axis=0)
    lower = jnp.concatenate([zero, field[:-1]], axis=0)
    return upper - lower


def edge_rows(p, across, fields, dim):
    n = p.shape[dim]
    take = lambda f, i: lax.index_in_dim(f, i, axis=dim, keepdims=False)
    high = [take(p, n - 2), take(p, n - 1), take(across, n - 1)] + [take(f, n - 1) for f in fields]
    low = [take(p, 1), take(p, 0), take(across, 0)] + [take(f, 0) for f in fields]
    return jnp.stack(high), jnp.stack(low)


def substep_kernel(flags, winds, thermo, heat, from_xm, from_xp, from_ym, from_yp, winds_out, thermo_out):
    levels, nx, ny = heat.shape
    row = lax.broadcasted_iota(jnp.int32, (nx, ny), 0)
    lane = lax.broadcasted_iota(jnp.int32, (nx, ny), 1)
    wide = lambda a: jnp.broadcast_to(a, (nx, ny))
    x_up = lambda f, h: jnp.where(row == nx - 1, wide(h), pltpu.roll(f, nx - 1, 0))
    x_dn = lambda f, h: jnp.where(row == 0, wide(h), pltpu.roll(f, 1, 0))
    y_up = lambda f, h: jnp.where(lane == ny - 1, wide(h), pltpu.roll(f, ny - 1, 1))
    y_dn = lambda f, h: jnp.where(lane == 0, wide(h), pltpu.roll(f, 1, 1))
    xm = lambda i, k: from_xm[i, k : k + 1, :]
    xp = lambda i, k: from_xp[i, k : k + 1, :]
    ym = lambda i, k: from_ym[i, :, k : k + 1]
    yp = lambda i, k: from_yp[i, :, k : k + 1]

    def vert(ref, k):
        upper = ref[k + 1] if k + 1 < levels else jnp.zeros((nx, ny), jnp.float32)
        lower = ref[k - 1] if k > 0 else jnp.zeros((nx, ny), jnp.float32)
        return upper - lower

    press = thermo.at[0]
    for k in range(levels):
        p = press[k]
        theta = thermo[1, k]
        winds_out[0, k] = winds[0, k] - 0.25 * (x_up(p, xp(1, k)) - x_dn(p, xm(1, k)))
        winds_out[1, k] = winds[1, k] - 0.25 * (y_up(p, yp(1, k)) - y_dn(p, ym(1, k)))
        up_n = winds[2, k] - 0.25 * vert(press, k) + 0.1 * theta
        winds_out[2, k] = up_n
        for index in (1, 2):
            field = thermo[index, k]
            east_c = x_up(field, xp(index + 2, k))
            west_c = x_dn(field, xm(index + 2, k))
            lap = east_c + west_c + y_up(field, yp(index + 2, k)) + y_dn(field, ym(index + 2, k)) - 4.0 * field
            new = field + 0.1 * lap - 0.15 * (east_c - west_c)
            if index == 1:
                new = new - 0.1 * up_n + heat[k]
            thermo_out[index, k] = new
    up_out = winds_out.at[2]
    for k in range(levels):
        p = press[k]
        east_hi = xp(2, k) - 0.25 * (xp(0, k) - p[nx - 1 : nx, :])
        east_lo = xm(2, k) - 0.25 * (p[0:1, :] - xm(0, k))
        north_hi = yp(2, k) - 0.25 * (yp(0, k) - p[:, ny - 1 : ny])
        north_lo = ym(2, k) - 0.25 * (p[:, 0:1] - ym(0, k))
        east_hi = jnp.where(flags[1] == 1, 0.0, east_hi)
        east_lo = jnp.where(flags[0] == 1, 0.0, east_lo)
        north_hi = jnp.where(flags[3] == 1, 0.0, north_hi)
        north_lo = jnp.where(flags[2] == 1, 0.0, north_lo)
        east_n = winds_out[0, k]
        north_n = winds_out[1, k]
        diverge = (x_up(east_n, east_hi) - x_dn(east_n, east_lo)) + (
            y_up(north_n, north_hi) - y_dn(north_n, north_lo)
        )
        thermo_out[0, k] = p - 0.25 * (diverge + vert(up_out, k))


def substep(winds, thermo, halos, heat_term, flags):
    vmem = pl.BlockSpec(memory_space=pltpu.VMEM)
    return pl.pallas_call(
        substep_kernel,
        out_shape=(
            jax.ShapeDtypeStruct(winds.shape, jnp.float32),
            jax.ShapeDtypeStruct(thermo.shape, jnp.float32),
        ),
        in_specs=[pl.BlockSpec(memory_space=pltpu.SMEM)] + [vmem] * 7,
        out_specs=(vmem, vmem),
    )(flags, winds, thermo, heat_term, *halos)


def per_device(winds, thermo, terrain, shadow_len, sector, land_mask):
    cols_x, cols_y = terrain.shape
    levels = winds.shape[1]
    nxd = lax.axis_size("gx")
    nyd = lax.axis_size("gy")
    ix = lax.axis_index("gx")
    iy = lax.axis_index("gy")
    first_x, last_x = ix == 0, ix == nxd - 1
    first_y, last_y = iy == 0, iy == nyd - 1
    ramp = (ramp_rate * jnp.arange(cols_x).astype(jnp.float32) / cols_x)[:, None]
    west_terms = jnp.exp(terrain + ramp) * (shade_scale / cols_x)
    east_terms = jnp.exp(terrain - ramp) * (shade_scale / cols_x)
    prefix = jnp.cumsum(west_terms, axis=0) - west_terms
    west_tot = jnp.sum(west_terms, axis=0)
    east_tot = jnp.sum(east_terms, axis=0)
    suffix = east_tot[None, :] - jnp.cumsum(east_terms, axis=0)

    flags = jnp.stack([first_x, last_x, first_y, last_y]).astype(jnp.int32)
    far = {}
    for step in range(ITERS):
        east_v, north_v, up_v, press, theta, moist = (winds[0], winds[1], winds[2], thermo[0], thermo[1], thermo[2])
        to_xp, to_xm = edge_rows(press, east_v, (theta, moist), 1)
        to_yp, to_ym = edge_rows(press, north_v, (theta, moist), 2)
        to_yp = jnp.swapaxes(to_yp, 1, 2)
        to_ym = jnp.swapaxes(to_ym, 1, 2)
        if step == 0:
            to_xp = jnp.concatenate([to_xp.reshape(-1, cols_y), west_tot[None]], axis=0)
            to_xm = jnp.concatenate([to_xm.reshape(-1, cols_y), east_tot[None]], axis=0)
        from_xm = shifted(to_xp, "gx", 1)
        from_xp = shifted(to_xm, "gx", -1)
        from_ym = shifted(to_yp, "gy", 1)
        from_yp = shifted(to_ym, "gy", -1)
        if step == 0:
            near_w = shifted(west_tot, "gx", 2)
            near_e = shifted(east_tot, "gx", -2)
            far[("w", 1)] = from_xm[-1]
            far[("e", 1)] = from_xp[-1]
            far[("w", 2)] = near_w
            far[("e", 2)] = near_e
            relay_w = shifted(jnp.stack([far[("w", 1)], near_w]), "gx", 2)
            relay_e = shifted(jnp.stack([far[("e", 1)], near_e]), "gx", -2)
            far[("w", 3)], far[("w", 4)] = relay_w[0], relay_w[1]
            far[("e", 3)], far[("e", 4)] = relay_e[0], relay_e[1]
            from_xm = from_xm[:-1].reshape(5, levels, cols_y)
            from_xp = from_xp[:-1].reshape(5, levels, cols_y)
            west_far = jnp.zeros((cols_y,), jnp.float32)
            east_far = jnp.zeros((cols_y,), jnp.float32)
            for reach in range(1, LMAX + 1):
                weight = jnp.where(shadow_len >= reach, math.exp(-decay_rate * reach), 0.0)
                west_far = west_far + weight * far[("w", reach)]
                east_far = east_far + weight * far[("e", reach)]
            west_occ = (prefix + west_far[None, :]) * jnp.exp(-terrain - ramp)
            east_occ = (suffix + east_far[None, :]) * jnp.exp(ramp - terrain)
            sun = jnp.where(sector[None, :] == 0, 1.0 / (1.0 + west_occ), 1.0 / (1.0 + east_occ))
            sky = 1.0 / (1.0 + 0.5 * (west_occ + east_occ))
            land = land_mask[0, 0].astype(jnp.float32)
            heating = land * (0.7 * sun + 0.3 * sky) + (1.0 - land) * 0.3 * sky
            profile = jnp.exp(-jnp.arange(levels).astype(jnp.float32) / 4.0)
            heat_term = profile[:, None, None] * heating[None]
        halos = (from_xm, from_xp, from_ym, from_yp)
        winds, thermo = substep(winds, thermo, halos, heat_term, flags)
    return (winds, thermo)


def solution(mesh):
    return jax.shard_map(
        per_device,
        mesh=mesh,
        in_specs=(
            P(None, None, "gx", "gy"),
            P(None, None, "gx", "gy"),
            P("gx", "gy"),
            P("gy"),
            P("gy"),
            P("gx", "gy"),
        ),
        out_specs=(P(None, None, "gx", "gy"), P(None, None, "gx", "gy")),
        check_vma=False,
    )
```

```python
import math

import jax
import jax.numpy as jnp
from jax import lax
from jax.experimental import pallas as pl
from jax.experimental.pallas import tpu as pltpu
from jax.sharding import PartitionSpec as P

ITERS = 2
LMAX = 4


ramp_rate = 0.7
decay_rate = 0.25
shade_scale = 0.1


def shifted(block, axis, distance):
    devices = range(lax.axis_size(axis))
    route = [(i, i + distance) for i in devices if i + distance in devices]
    return lax.ppermute(block, axis, route)


def vertical(field):
    zero = jnp.zeros((1,) + field.shape[1:], jnp.float32)
    upper = jnp.concatenate([field[1:], zero], axis=0)
    lower = jnp.concatenate([zero, field[:-1]], axis=0)
    return upper - lower


KPAD = 32


def pack_halos(levels, tile, to_xp, to_xm, to_yp, to_ym):
    nx, ny = to_yp.shape[1], to_yp.shape[2]
    lane = lax.broadcasted_iota(jnp.int32, (nx, ny), 1)
    hi_x = (("p", nx - 2), ("p", nx - 1), ("u", nx - 1), ("th", nx - 1), ("q", nx - 1))
    lo_x = (("p", 1), ("p", 0), ("u", 0), ("th", 0), ("q", 0))
    hi_y = (("p", ny - 2), ("p", ny - 1), ("v", ny - 1), ("th", ny - 1), ("q", ny - 1))
    lo_y = (("p", 1), ("p", 0), ("v", 0), ("th", 0), ("q", 0))
    acc_hi = [jnp.zeros((nx, ny), jnp.float32) for _ in hi_y]
    acc_lo = [jnp.zeros((nx, ny), jnp.float32) for _ in lo_y]
    for k in range(levels):
        for i, (name, r) in enumerate(hi_x):
            to_xp[i, k : k + 1, :] = tile(name, k)[r : r + 1, :]
        for i, (name, r) in enumerate(lo_x):
            to_xm[i, k : k + 1, :] = tile(name, k)[r : r + 1, :]
        for i, (name, c) in enumerate(hi_y):
            col = jnp.broadcast_to(tile(name, k)[:, c : c + 1], (nx, ny))
            acc_hi[i] = jnp.where(lane == k, col, acc_hi[i])
        for i, (name, c) in enumerate(lo_y):
            col = jnp.broadcast_to(tile(name, k)[:, c : c + 1], (nx, ny))
            acc_lo[i] = jnp.where(lane == k, col, acc_lo[i])
    for i in range(len(hi_y)):
        to_yp[i] = acc_hi[i]
        to_ym[i] = acc_lo[i]


def state_tile(winds, thermo):
    refs = {"u": winds.at[0], "v": winds.at[1], "p": thermo.at[0], "th": thermo.at[1], "q": thermo.at[2]}
    return lambda name, k: refs[name][k]


def pack_kernel(tots, winds, thermo, to_xp, to_xm, to_yp, to_ym):
    levels = winds.shape[1]
    to_xp[...] = jnp.zeros(to_xp.shape, jnp.float32)
    to_xm[...] = jnp.zeros(to_xm.shape, jnp.float32)
    pack_halos(levels, state_tile(winds, thermo), to_xp, to_xm, to_yp, to_ym)
    to_xp[0, levels : levels + 1, :] = tots[0:1, :]
    to_xm[0, levels : levels + 1, :] = tots[1:2, :]


def substep_kernel(flags, winds, thermo, heat, from_xm, from_xp, from_ym, from_yp, winds_out, thermo_out, *sends):
    levels, nx, ny = heat.shape
    row = lax.broadcasted_iota(jnp.int32, (nx, ny), 0)
    lane = lax.broadcasted_iota(jnp.int32, (nx, ny), 1)
    wide = lambda a: jnp.broadcast_to(a, (nx, ny))
    x_up = lambda f, h: jnp.where(row == nx - 1, wide(h), pltpu.roll(f, nx - 1, 0))
    x_dn = lambda f, h: jnp.where(row == 0, wide(h), pltpu.roll(f, 1, 0))
    y_up = lambda f, h: jnp.where(lane == ny - 1, wide(h), pltpu.roll(f, ny - 1, 1))
    y_dn = lambda f, h: jnp.where(lane == 0, wide(h), pltpu.roll(f, 1, 1))
    xm = lambda i, k: from_xm[i, k : k + 1, :]
    xp = lambda i, k: from_xp[i, k : k + 1, :]
    ym = lambda i, k: from_ym[i, :, k : k + 1]
    yp = lambda i, k: from_yp[i, :, k : k + 1]

    def vert(ref, k):
        upper = ref[k + 1] if k + 1 < levels else jnp.zeros((nx, ny), jnp.float32)
        lower = ref[k - 1] if k > 0 else jnp.zeros((nx, ny), jnp.float32)
        return upper - lower

    press = thermo.at[0]
    for k in range(levels):
        p = press[k]
        theta = thermo[1, k]
        winds_out[0, k] = winds[0, k] - 0.25 * (x_up(p, xp(1, k)) - x_dn(p, xm(1, k)))
        winds_out[1, k] = winds[1, k] - 0.25 * (y_up(p, yp(1, k)) - y_dn(p, ym(1, k)))
        up_n = winds[2, k] - 0.25 * vert(press, k) + 0.1 * theta
        winds_out[2, k] = up_n
        for index in (1, 2):
            field = thermo[index, k]
            east_c = x_up(field, xp(index + 2, k))
            west_c = x_dn(field, xm(index + 2, k))
            lap = east_c + west_c + y_up(field, yp(index + 2, k)) + y_dn(field, ym(index + 2, k)) - 4.0 * field
            new = field + 0.1 * lap - 0.15 * (east_c - west_c)
            if index == 1:
                new = new - 0.1 * up_n + heat[k]
            thermo_out[index, k] = new
    up_out = winds_out.at[2]
    for k in range(levels):
        p = press[k]
        east_hi = xp(2, k) - 0.25 * (xp(0, k) - p[nx - 1 : nx, :])
        east_lo = xm(2, k) - 0.25 * (p[0:1, :] - xm(0, k))
        north_hi = yp(2, k) - 0.25 * (yp(0, k) - p[:, ny - 1 : ny])
        north_lo = ym(2, k) - 0.25 * (p[:, 0:1] - ym(0, k))
        east_hi = jnp.where(flags[1] == 1, 0.0, east_hi)
        east_lo = jnp.where(flags[0] == 1, 0.0, east_lo)
        north_hi = jnp.where(flags[3] == 1, 0.0, north_hi)
        north_lo = jnp.where(flags[2] == 1, 0.0, north_lo)
        east_n = winds_out[0, k]
        north_n = winds_out[1, k]
        diverge = (x_up(east_n, east_hi) - x_dn(east_n, east_lo)) + (
            y_up(north_n, north_hi) - y_dn(north_n, north_lo)
        )
        thermo_out[0, k] = p - 0.25 * (diverge + vert(up_out, k))
    if sends:
        to_xp, to_xm, to_yp, to_ym = sends
        to_xp[...] = jnp.zeros(to_xp.shape, jnp.float32)
        to_xm[...] = jnp.zeros(to_xm.shape, jnp.float32)
        pack_halos(levels, state_tile(winds_out, thermo_out), to_xp, to_xm, to_yp, to_ym)


def halo_shapes(winds):
    _, levels, nx, ny = winds.shape
    x_msg = jax.ShapeDtypeStruct((5, KPAD, ny), jnp.float32)
    y_msg = jax.ShapeDtypeStruct((5, nx, ny), jnp.float32)
    return (x_msg, x_msg, y_msg, y_msg)


VMEM = pl.BlockSpec(memory_space=pltpu.VMEM)


def pack(winds, thermo, tots):
    return pl.pallas_call(
        pack_kernel,
        out_shape=halo_shapes(winds),
        in_specs=[VMEM] * 3,
        out_specs=(VMEM,) * 4,
    )(tots, winds, thermo)


def substep(winds, thermo, halos, heat_term, flags, emit):
    outs = (
        jax.ShapeDtypeStruct(winds.shape, jnp.float32),
        jax.ShapeDtypeStruct(thermo.shape, jnp.float32),
    )
    if emit:
        outs = outs + halo_shapes(winds)
    return pl.pallas_call(
        substep_kernel,
        out_shape=outs,
        in_specs=[pl.BlockSpec(memory_space=pltpu.SMEM)] + [VMEM] * 7,
        out_specs=(VMEM,) * len(outs),
    )(flags, winds, thermo, heat_term, *halos)


def per_device(winds, thermo, terrain, shadow_len, sector, land_mask):
    cols_x, cols_y = terrain.shape
    levels = winds.shape[1]
    nxd = lax.axis_size("gx")
    nyd = lax.axis_size("gy")
    ix = lax.axis_index("gx")
    iy = lax.axis_index("gy")
    first_x, last_x = ix == 0, ix == nxd - 1
    first_y, last_y = iy == 0, iy == nyd - 1
    ramp = (ramp_rate * jnp.arange(cols_x).astype(jnp.float32) / cols_x)[:, None]
    west_terms = jnp.exp(terrain + ramp) * (shade_scale / cols_x)
    east_terms = jnp.exp(terrain - ramp) * (shade_scale / cols_x)
    prefix = jnp.cumsum(west_terms, axis=0) - west_terms
    west_tot = jnp.sum(west_terms, axis=0)
    east_tot = jnp.sum(east_terms, axis=0)
    suffix = east_tot[None, :] - jnp.cumsum(east_terms, axis=0)

    flags = jnp.stack([first_x, last_x, first_y, last_y]).astype(jnp.int32)
    to_xp, to_xm, to_yp, to_ym = pack(winds, thermo, jnp.stack([west_tot, east_tot]))
    far = {}
    for step in range(ITERS):
        from_xm = shifted(to_xp, "gx", 1)
        from_xp = shifted(to_xm, "gx", -1)
        from_ym = shifted(to_yp, "gy", 1)
        from_yp = shifted(to_ym, "gy", -1)
        if step == 0:
            near_w = shifted(west_tot, "gx", 2)
            near_e = shifted(east_tot, "gx", -2)
            far[("w", 1)] = from_xm[0, levels]
            far[("e", 1)] = from_xp[0, levels]
            far[("w", 2)] = near_w
            far[("e", 2)] = near_e
            relay_w = shifted(jnp.stack([far[("w", 1)], near_w]), "gx", 2)
            relay_e = shifted(jnp.stack([far[("e", 1)], near_e]), "gx", -2)
            far[("w", 3)], far[("w", 4)] = relay_w[0], relay_w[1]
            far[("e", 3)], far[("e", 4)] = relay_e[0], relay_e[1]
            west_far = jnp.zeros((cols_y,), jnp.float32)
            east_far = jnp.zeros((cols_y,), jnp.float32)
            for reach in range(1, LMAX + 1):
                weight = jnp.where(shadow_len >= reach, math.exp(-decay_rate * reach), 0.0)
                west_far = west_far + weight * far[("w", reach)]
                east_far = east_far + weight * far[("e", reach)]
            west_occ = (prefix + west_far[None, :]) * jnp.exp(-terrain - ramp)
            east_occ = (suffix + east_far[None, :]) * jnp.exp(ramp - terrain)
            sun = jnp.where(sector[None, :] == 0, 1.0 / (1.0 + west_occ), 1.0 / (1.0 + east_occ))
            sky = 1.0 / (1.0 + 0.5 * (west_occ + east_occ))
            land = land_mask[0, 0].astype(jnp.float32)
            heating = land * (0.7 * sun + 0.3 * sky) + (1.0 - land) * 0.3 * sky
            profile = jnp.exp(-jnp.arange(levels).astype(jnp.float32) / 4.0)
            heat_term = profile[:, None, None] * heating[None]
        halos = (from_xm, from_xp, from_ym, from_yp)
        emit = step + 1 < ITERS
        outs = substep(winds, thermo, halos, heat_term, flags, emit)
        winds, thermo = outs[0], outs[1]
        if emit:
            to_xp, to_xm, to_yp, to_ym = outs[2:]
    return (winds, thermo)


def solution(mesh):
    return jax.shard_map(
        per_device,
        mesh=mesh,
        in_specs=(
            P(None, None, "gx", "gy"),
            P(None, None, "gx", "gy"),
            P("gx", "gy"),
            P("gy"),
            P("gy"),
            P("gx", "gy"),
        ),
        out_specs=(P(None, None, "gx", "gy"), P(None, None, "gx", "gy")),
        check_vma=False,
    )
```

```python
import math

import jax
import jax.numpy as jnp
from jax import lax
from jax.experimental import pallas as pl
from jax.experimental.pallas import tpu as pltpu
from jax.sharding import PartitionSpec as P

ITERS = 2
LMAX = 4


ramp_rate = 0.7
decay_rate = 0.25
shade_scale = 0.1


def shifted(block, axis, distance):
    devices = range(lax.axis_size(axis))
    route = [(i, i + distance) for i in devices if i + distance in devices]
    return lax.ppermute(block, axis, route)


def vertical(field):
    zero = jnp.zeros((1,) + field.shape[1:], jnp.float32)
    upper = jnp.concatenate([field[1:], zero], axis=0)
    lower = jnp.concatenate([zero, field[:-1]], axis=0)
    return upper - lower


KPAD = 32


def rolled(a, shift, axis):
    shift %= a.shape[axis]
    return pltpu.roll(a, shift, axis) if shift else a


def pack_halos(levels, tile, to_xp, to_xm, to_yp, to_ym):
    nx, ny = to_yp.shape[1], to_yp.shape[2]
    row = lax.broadcasted_iota(jnp.int32, (nx, ny), 0)
    lane = lax.broadcasted_iota(jnp.int32, (nx, ny), 1)
    hi_x = (("p", nx - 2), ("p", nx - 1), ("u", nx - 1), ("th", nx - 1), ("q", nx - 1))
    lo_x = (("p", 1), ("p", 0), ("u", 0), ("th", 0), ("q", 0))
    hi_y = (("p", ny - 2), ("p", ny - 1), ("v", ny - 1), ("th", ny - 1), ("q", ny - 1))
    lo_y = (("p", 1), ("p", 0), ("v", 0), ("th", 0), ("q", 0))
    zero = jnp.zeros((nx, ny), jnp.float32)
    for spec, to_y in ((hi_y, to_yp), (lo_y, to_ym)):
        for i, (name, c) in enumerate(spec):
            acc = zero
            for k in range(levels):
                acc = jnp.where(lane == k, rolled(tile(name, k), k - c, 1), acc)
            to_y[i] = acc
    for spec, to_x in ((hi_x, to_xp), (lo_x, to_xm)):
        for i, (name, r) in enumerate(spec):
            for g in range(KPAD // nx):
                acc = zero
                for k in range(g * nx, min(levels, (g + 1) * nx)):
                    acc = jnp.where(row == k % nx, rolled(tile(name, k), k - r, 0), acc)
                to_x[i, g * nx : (g + 1) * nx, :] = acc


def state_tile(winds, thermo):
    refs = {"u": winds.at[0], "v": winds.at[1], "p": thermo.at[0], "th": thermo.at[1], "q": thermo.at[2]}
    return lambda name, k: refs[name][k]


def pack_kernel(tots, winds, thermo, to_xp, to_xm, to_yp, to_ym):
    levels = winds.shape[1]
    pack_halos(levels, state_tile(winds, thermo), to_xp, to_xm, to_yp, to_ym)
    to_xp[0, levels : levels + 1, :] = tots[0:1, :]
    to_xm[0, levels : levels + 1, :] = tots[1:2, :]


def substep_kernel(flags, winds, thermo, heat, from_xm, from_xp, from_ym, from_yp, winds_out, thermo_out, *sends):
    levels, nx, ny = heat.shape
    row = lax.broadcasted_iota(jnp.int32, (nx, ny), 0)
    lane = lax.broadcasted_iota(jnp.int32, (nx, ny), 1)
    xm = lambda i, k: rolled(from_xm[i, (k // nx) * nx : (k // nx + 1) * nx, :], -k, 0)
    xp = lambda i, k: rolled(from_xp[i, (k // nx) * nx : (k // nx + 1) * nx, :], nx - 1 - k, 0)
    ym = lambda i, k: rolled(from_ym[i], -k, 1)
    yp = lambda i, k: rolled(from_yp[i], ny - 1 - k, 1)
    x_up = lambda f, h: jnp.where(row == nx - 1, h, pltpu.roll(f, nx - 1, 0))
    x_dn = lambda f, h: jnp.where(row == 0, h, pltpu.roll(f, 1, 0))
    y_up = lambda f, h: jnp.where(lane == ny - 1, h, pltpu.roll(f, ny - 1, 1))
    y_dn = lambda f, h: jnp.where(lane == 0, h, pltpu.roll(f, 1, 1))

    def vert(ref, k):
        upper = ref[k + 1] if k + 1 < levels else jnp.zeros((nx, ny), jnp.float32)
        lower = ref[k - 1] if k > 0 else jnp.zeros((nx, ny), jnp.float32)
        return upper - lower

    press = thermo.at[0]
    for k in range(levels):
        p = press[k]
        theta = thermo[1, k]
        winds_out[0, k] = winds[0, k] - 0.25 * (x_up(p, xp(1, k)) - x_dn(p, xm(1, k)))
        winds_out[1, k] = winds[1, k] - 0.25 * (y_up(p, yp(1, k)) - y_dn(p, ym(1, k)))
        up_n = winds[2, k] - 0.25 * vert(press, k) + 0.1 * theta
        winds_out[2, k] = up_n
        for index in (1, 2):
            field = thermo[index, k]
            east_c = x_up(field, xp(index + 2, k))
            west_c = x_dn(field, xm(index + 2, k))
            lap = east_c + west_c + y_up(field, yp(index + 2, k)) + y_dn(field, ym(index + 2, k)) - 4.0 * field
            new = field + 0.1 * lap - 0.15 * (east_c - west_c)
            if index == 1:
                new = new - 0.1 * up_n + heat[k]
            thermo_out[index, k] = new
    up_out = winds_out.at[2]
    for k in range(levels):
        p = press[k]
        east_hi = xp(2, k) - 0.25 * (xp(0, k) - p)
        east_lo = xm(2, k) - 0.25 * (p - xm(0, k))
        north_hi = yp(2, k) - 0.25 * (yp(0, k) - p)
        north_lo = ym(2, k) - 0.25 * (p - ym(0, k))
        east_hi = jnp.where(flags[1] == 1, 0.0, east_hi)
        east_lo = jnp.where(flags[0] == 1, 0.0, east_lo)
        north_hi = jnp.where(flags[3] == 1, 0.0, north_hi)
        north_lo = jnp.where(flags[2] == 1, 0.0, north_lo)
        east_n = winds_out[0, k]
        north_n = winds_out[1, k]
        diverge = (x_up(east_n, east_hi) - x_dn(east_n, east_lo)) + (
            y_up(north_n, north_hi) - y_dn(north_n, north_lo)
        )
        thermo_out[0, k] = p - 0.25 * (diverge + vert(up_out, k))
    if sends:
        pack_halos(levels, state_tile(winds_out, thermo_out), *sends)


def halo_shapes(winds):
    _, levels, nx, ny = winds.shape
    x_msg = jax.ShapeDtypeStruct((5, KPAD, ny), jnp.float32)
    y_msg = jax.ShapeDtypeStruct((5, nx, ny), jnp.float32)
    return (x_msg, x_msg, y_msg, y_msg)


VMEM = pl.BlockSpec(memory_space=pltpu.VMEM)


def pack(winds, thermo, tots):
    return pl.pallas_call(
        pack_kernel,
        out_shape=halo_shapes(winds),
        in_specs=[VMEM] * 3,
        out_specs=(VMEM,) * 4,
    )(tots, winds, thermo)


def substep(winds, thermo, halos, heat_term, flags, emit):
    outs = (
        jax.ShapeDtypeStruct(winds.shape, jnp.float32),
        jax.ShapeDtypeStruct(thermo.shape, jnp.float32),
    )
    if emit:
        outs = outs + halo_shapes(winds)
    return pl.pallas_call(
        substep_kernel,
        out_shape=outs,
        in_specs=[pl.BlockSpec(memory_space=pltpu.SMEM)] + [VMEM] * 7,
        out_specs=(VMEM,) * len(outs),
    )(flags, winds, thermo, heat_term, *halos)


def per_device(winds, thermo, terrain, shadow_len, sector, land_mask):
    cols_x, cols_y = terrain.shape
    levels = winds.shape[1]
    nxd = lax.axis_size("gx")
    nyd = lax.axis_size("gy")
    ix = lax.axis_index("gx")
    iy = lax.axis_index("gy")
    first_x, last_x = ix == 0, ix == nxd - 1
    first_y, last_y = iy == 0, iy == nyd - 1
    ramp = (ramp_rate * jnp.arange(cols_x).astype(jnp.float32) / cols_x)[:, None]
    west_terms = jnp.exp(terrain + ramp) * (shade_scale / cols_x)
    east_terms = jnp.exp(terrain - ramp) * (shade_scale / cols_x)
    prefix = jnp.cumsum(west_terms, axis=0) - west_terms
    west_tot = jnp.sum(west_terms, axis=0)
    east_tot = jnp.sum(east_terms, axis=0)
    suffix = east_tot[None, :] - jnp.cumsum(east_terms, axis=0)

    flags = jnp.stack([first_x, last_x, first_y, last_y]).astype(jnp.int32)
    to_xp, to_xm, to_yp, to_ym = pack(winds, thermo, jnp.stack([west_tot, east_tot]))
    far = {}
    for step in range(ITERS):
        from_xm = shifted(to_xp, "gx", 1)
        from_xp = shifted(to_xm, "gx", -1)
        from_ym = shifted(to_yp, "gy", 1)
        from_yp = shifted(to_ym, "gy", -1)
        if step == 0:
            near_w = shifted(west_tot, "gx", 2)
            near_e = shifted(east_tot, "gx", -2)
            far[("w", 1)] = from_xm[0, levels]
            far[("e", 1)] = from_xp[0, levels]
            far[("w", 2)] = near_w
            far[("e", 2)] = near_e
            relay_w = shifted(jnp.stack([far[("w", 1)], near_w]), "gx", 2)
            relay_e = shifted(jnp.stack([far[("e", 1)], near_e]), "gx", -2)
            far[("w", 3)], far[("w", 4)] = relay_w[0], relay_w[1]
            far[("e", 3)], far[("e", 4)] = relay_e[0], relay_e[1]
            west_far = jnp.zeros((cols_y,), jnp.float32)
            east_far = jnp.zeros((cols_y,), jnp.float32)
            for reach in range(1, LMAX + 1):
                weight = jnp.where(shadow_len >= reach, math.exp(-decay_rate * reach), 0.0)
                west_far = west_far + weight * far[("w", reach)]
                east_far = east_far + weight * far[("e", reach)]
            west_occ = (prefix + west_far[None, :]) * jnp.exp(-terrain - ramp)
            east_occ = (suffix + east_far[None, :]) * jnp.exp(ramp - terrain)
            sun = jnp.where(sector[None, :] == 0, 1.0 / (1.0 + west_occ), 1.0 / (1.0 + east_occ))
            sky = 1.0 / (1.0 + 0.5 * (west_occ + east_occ))
            land = land_mask[0, 0].astype(jnp.float32)
            heating = land * (0.7 * sun + 0.3 * sky) + (1.0 - land) * 0.3 * sky
            profile = jnp.exp(-jnp.arange(levels).astype(jnp.float32) / 4.0)
            heat_term = profile[:, None, None] * heating[None]
        halos = (from_xm, from_xp, from_ym, from_yp)
        emit = step + 1 < ITERS
        outs = substep(winds, thermo, halos, heat_term, flags, emit)
        winds, thermo = outs[0], outs[1]
        if emit:
            to_xp, to_xm, to_yp, to_ym = outs[2:]
    return (winds, thermo)


def solution(mesh):
    return jax.shard_map(
        per_device,
        mesh=mesh,
        in_specs=(
            P(None, None, "gx", "gy"),
            P(None, None, "gx", "gy"),
            P("gx", "gy"),
            P("gy"),
            P("gy"),
            P("gx", "gy"),
        ),
        out_specs=(P(None, None, "gx", "gy"), P(None, None, "gx", "gy")),
        check_vma=False,
    )
```

```python
import functools
import math

import jax
import jax.numpy as jnp
from jax import lax
from jax.experimental import pallas as pl
from jax.experimental.pallas import tpu as pltpu
from jax.sharding import PartitionSpec as P

ITERS = 2
LMAX = 4


ramp_rate = 0.7
decay_rate = 0.25
shade_scale = 0.1


def shifted(block, axis, distance):
    devices = range(lax.axis_size(axis))
    route = [(i, i + distance) for i in devices if i + distance in devices]
    return lax.ppermute(block, axis, route)


def vertical(field):
    zero = jnp.zeros((1,) + field.shape[1:], jnp.float32)
    upper = jnp.concatenate([field[1:], zero], axis=0)
    lower = jnp.concatenate([zero, field[:-1]], axis=0)
    return upper - lower


KPAD = 32


def rolled(a, shift, axis):
    shift %= a.shape[axis]
    return pltpu.roll(a, shift, axis) if shift else a


def pack_halos(levels, tile, to_xp, to_xm, to_yp, to_ym):
    nx, ny = to_yp.shape[1], to_yp.shape[2]
    row = lax.broadcasted_iota(jnp.int32, (nx, ny), 0)
    lane = lax.broadcasted_iota(jnp.int32, (nx, ny), 1)
    hi_x = (("p", nx - 2), ("p", nx - 1), ("u", nx - 1), ("th", nx - 1), ("q", nx - 1))
    lo_x = (("p", 1), ("p", 0), ("u", 0), ("th", 0), ("q", 0))
    hi_y = (("p", ny - 2), ("p", ny - 1), ("v", ny - 1), ("th", ny - 1), ("q", ny - 1))
    lo_y = (("p", 1), ("p", 0), ("v", 0), ("th", 0), ("q", 0))
    zero = jnp.zeros((nx, ny), jnp.float32)
    for spec, to_y in ((hi_y, to_yp), (lo_y, to_ym)):
        for i, (name, c) in enumerate(spec):
            acc = zero
            for k in range(levels):
                acc = jnp.where(lane == k, rolled(tile(name, k), k - c, 1), acc)
            to_y[i] = acc
    for spec, to_x in ((hi_x, to_xp), (lo_x, to_xm)):
        for i, (name, r) in enumerate(spec):
            for g in range(KPAD // nx):
                acc = zero
                for k in range(g * nx, min(levels, (g + 1) * nx)):
                    acc = jnp.where(row == k % nx, rolled(tile(name, k), k - r, 0), acc)
                to_x[i, g * nx : (g + 1) * nx, :] = acc


def state_tile(winds, thermo):
    refs = {"u": winds.at[0], "v": winds.at[1], "p": thermo.at[0], "th": thermo.at[1], "q": thermo.at[2]}
    return lambda name, k: refs[name][k]


def pack_kernel(tots, winds, thermo, to_xp, to_xm, to_yp, to_ym):
    levels = winds.shape[1]
    pack_halos(levels, state_tile(winds, thermo), to_xp, to_xm, to_yp, to_ym)
    to_xp[0, levels : levels + 1, :] = tots[0:1, :]
    to_xm[0, levels : levels + 1, :] = tots[1:2, :]


def substep_kernel(devices, profile, winds, thermo, heating, from_xm, from_xp, from_ym, from_yp, winds_out, thermo_out, *sends):
    levels, nx, ny = winds.shape[1:]
    ix, iy = lax.axis_index("gx"), lax.axis_index("gy")
    edge = (ix == 0, ix == devices[0] - 1, iy == 0, iy == devices[1] - 1)
    row = lax.broadcasted_iota(jnp.int32, (nx, ny), 0)
    lane = lax.broadcasted_iota(jnp.int32, (nx, ny), 1)
    xm = lambda i, k: rolled(from_xm[i, (k // nx) * nx : (k // nx + 1) * nx, :], -k, 0)
    xp = lambda i, k: rolled(from_xp[i, (k // nx) * nx : (k // nx + 1) * nx, :], nx - 1 - k, 0)
    ym = lambda i, k: rolled(from_ym[i], -k, 1)
    yp = lambda i, k: rolled(from_yp[i], ny - 1 - k, 1)
    x_up = lambda f, h: jnp.where(row == nx - 1, h, pltpu.roll(f, nx - 1, 0))
    x_dn = lambda f, h: jnp.where(row == 0, h, pltpu.roll(f, 1, 0))
    y_up = lambda f, h: jnp.where(lane == ny - 1, h, pltpu.roll(f, ny - 1, 1))
    y_dn = lambda f, h: jnp.where(lane == 0, h, pltpu.roll(f, 1, 1))

    def vert(ref, k):
        upper = ref[k + 1] if k + 1 < levels else jnp.zeros((nx, ny), jnp.float32)
        lower = ref[k - 1] if k > 0 else jnp.zeros((nx, ny), jnp.float32)
        return upper - lower

    press = thermo.at[0]
    for k in range(levels):
        p = press[k]
        theta = thermo[1, k]
        winds_out[0, k] = winds[0, k] - 0.25 * (x_up(p, xp(1, k)) - x_dn(p, xm(1, k)))
        winds_out[1, k] = winds[1, k] - 0.25 * (y_up(p, yp(1, k)) - y_dn(p, ym(1, k)))
        up_n = winds[2, k] - 0.25 * vert(press, k) + 0.1 * theta
        winds_out[2, k] = up_n
        for index in (1, 2):
            field = thermo[index, k]
            east_c = x_up(field, xp(index + 2, k))
            west_c = x_dn(field, xm(index + 2, k))
            lap = east_c + west_c + y_up(field, yp(index + 2, k)) + y_dn(field, ym(index + 2, k)) - 4.0 * field
            new = field + 0.1 * lap - 0.15 * (east_c - west_c)
            if index == 1:
                new = new - 0.1 * up_n + profile[k] * heating[...]
            thermo_out[index, k] = new
    up_out = winds_out.at[2]
    for k in range(levels):
        p = press[k]
        east_hi = xp(2, k) - 0.25 * (xp(0, k) - p)
        east_lo = xm(2, k) - 0.25 * (p - xm(0, k))
        north_hi = yp(2, k) - 0.25 * (yp(0, k) - p)
        north_lo = ym(2, k) - 0.25 * (p - ym(0, k))
        east_hi = jnp.where(edge[1], 0.0, east_hi)
        east_lo = jnp.where(edge[0], 0.0, east_lo)
        north_hi = jnp.where(edge[3], 0.0, north_hi)
        north_lo = jnp.where(edge[2], 0.0, north_lo)
        east_n = winds_out[0, k]
        north_n = winds_out[1, k]
        diverge = (x_up(east_n, east_hi) - x_dn(east_n, east_lo)) + (
            y_up(north_n, north_hi) - y_dn(north_n, north_lo)
        )
        thermo_out[0, k] = p - 0.25 * (diverge + vert(up_out, k))
    if sends:
        pack_halos(levels, state_tile(winds_out, thermo_out), *sends)


def halo_shapes(winds):
    _, levels, nx, ny = winds.shape
    x_msg = jax.ShapeDtypeStruct((5, KPAD, ny), jnp.float32)
    y_msg = jax.ShapeDtypeStruct((5, nx, ny), jnp.float32)
    return (x_msg, x_msg, y_msg, y_msg)


VMEM = pl.BlockSpec(memory_space=pltpu.VMEM)


def pack(winds, thermo, tots):
    return pl.pallas_call(
        pack_kernel,
        out_shape=halo_shapes(winds),
        in_specs=[VMEM] * 3,
        out_specs=(VMEM,) * 4,
    )(tots, winds, thermo)


def substep(winds, thermo, halos, profile, heating, emit):
    outs = (
        jax.ShapeDtypeStruct(winds.shape, jnp.float32),
        jax.ShapeDtypeStruct(thermo.shape, jnp.float32),
    )
    if emit:
        outs = outs + halo_shapes(winds)
    devices = (lax.axis_size("gx"), lax.axis_size("gy"))
    return pl.pallas_call(
        functools.partial(substep_kernel, devices),
        out_shape=outs,
        in_specs=[pl.BlockSpec(memory_space=pltpu.SMEM)] + [VMEM] * 7,
        out_specs=(VMEM,) * len(outs),
    )(profile, winds, thermo, heating, *halos)


def per_device(winds, thermo, terrain, shadow_len, sector, land_mask):
    cols_x, cols_y = terrain.shape
    levels = winds.shape[1]
    ramp = (ramp_rate * jnp.arange(cols_x).astype(jnp.float32) / cols_x)[:, None]
    west_terms = jnp.exp(terrain + ramp) * (shade_scale / cols_x)
    east_terms = jnp.exp(terrain - ramp) * (shade_scale / cols_x)
    prefix = jnp.cumsum(west_terms, axis=0) - west_terms
    west_tot = jnp.sum(west_terms, axis=0)
    east_tot = jnp.sum(east_terms, axis=0)
    suffix = east_tot[None, :] - jnp.cumsum(east_terms, axis=0)

    to_xp, to_xm, to_yp, to_ym = pack(winds, thermo, jnp.stack([west_tot, east_tot]))
    far = {}
    for step in range(ITERS):
        from_xm = shifted(to_xp, "gx", 1)
        from_xp = shifted(to_xm, "gx", -1)
        from_ym = shifted(to_yp, "gy", 1)
        from_yp = shifted(to_ym, "gy", -1)
        if step == 0:
            near_w = shifted(west_tot, "gx", 2)
            near_e = shifted(east_tot, "gx", -2)
            far[("w", 1)] = from_xm[0, levels]
            far[("e", 1)] = from_xp[0, levels]
            far[("w", 2)] = near_w
            far[("e", 2)] = near_e
            relay_w = shifted(jnp.stack([far[("w", 1)], near_w]), "gx", 2)
            relay_e = shifted(jnp.stack([far[("e", 1)], near_e]), "gx", -2)
            far[("w", 3)], far[("w", 4)] = relay_w[0], relay_w[1]
            far[("e", 3)], far[("e", 4)] = relay_e[0], relay_e[1]
            west_far = jnp.zeros((cols_y,), jnp.float32)
            east_far = jnp.zeros((cols_y,), jnp.float32)
            for reach in range(1, LMAX + 1):
                weight = jnp.where(shadow_len >= reach, math.exp(-decay_rate * reach), 0.0)
                west_far = west_far + weight * far[("w", reach)]
                east_far = east_far + weight * far[("e", reach)]
            west_occ = (prefix + west_far[None, :]) * jnp.exp(-terrain - ramp)
            east_occ = (suffix + east_far[None, :]) * jnp.exp(ramp - terrain)
            sun = jnp.where(sector[None, :] == 0, 1.0 / (1.0 + west_occ), 1.0 / (1.0 + east_occ))
            sky = 1.0 / (1.0 + 0.5 * (west_occ + east_occ))
            land = land_mask[0, 0].astype(jnp.float32)
            heating = land * (0.7 * sun + 0.3 * sky) + (1.0 - land) * 0.3 * sky
            profile = jnp.exp(-jnp.arange(levels).astype(jnp.float32) / 4.0)
        halos = (from_xm, from_xp, from_ym, from_yp)
        emit = step + 1 < ITERS
        outs = substep(winds, thermo, halos, profile, heating, emit)
        winds, thermo = outs[0], outs[1]
        if emit:
            to_xp, to_xm, to_yp, to_ym = outs[2:]
    return (winds, thermo)


def solution(mesh):
    return jax.shard_map(
        per_device,
        mesh=mesh,
        in_specs=(
            P(None, None, "gx", "gy"),
            P(None, None, "gx", "gy"),
            P("gx", "gy"),
            P("gy"),
            P("gy"),
            P("gx", "gy"),
        ),
        out_specs=(P(None, None, "gx", "gy"), P(None, None, "gx", "gy")),
        check_vma=False,
    )
```

```python
import functools
import math

import jax
import jax.numpy as jnp
from jax import lax
from jax.experimental import pallas as pl
from jax.experimental.pallas import tpu as pltpu
from jax.sharding import PartitionSpec as P

ITERS = 2
LMAX = 4


ramp_rate = 0.7
decay_rate = 0.25
shade_scale = 0.1


def shifted(block, axis, distance):
    devices = range(lax.axis_size(axis))
    route = [(i, i + distance) for i in devices if i + distance in devices]
    return lax.ppermute(block, axis, route)


def vertical(field):
    zero = jnp.zeros((1,) + field.shape[1:], jnp.float32)
    upper = jnp.concatenate([field[1:], zero], axis=0)
    lower = jnp.concatenate([zero, field[:-1]], axis=0)
    return upper - lower


KPAD = 32


def rolled(a, shift, axis):
    shift %= a.shape[axis]
    return pltpu.roll(a, shift, axis) if shift else a


def pack_halos(levels, tile, to_xp, to_xm, to_yp, to_ym, only=None):
    nx, ny = to_yp.shape[1], to_yp.shape[2]
    row = lax.broadcasted_iota(jnp.int32, (nx, ny), 0)
    lane = lax.broadcasted_iota(jnp.int32, (nx, ny), 1)
    hi_x = (("p", nx - 2), ("p", nx - 1), ("u", nx - 1), ("th", nx - 1), ("q", nx - 1))
    lo_x = (("p", 1), ("p", 0), ("u", 0), ("th", 0), ("q", 0))
    hi_y = (("p", ny - 2), ("p", ny - 1), ("v", ny - 1), ("th", ny - 1), ("q", ny - 1))
    lo_y = (("p", 1), ("p", 0), ("v", 0), ("th", 0), ("q", 0))
    zero = jnp.zeros((nx, ny), jnp.float32)
    for spec, to_y in ((hi_y, to_yp), (lo_y, to_ym)):
        for i, (name, c) in enumerate(spec):
            if only is not None and i != only:
                continue
            acc = zero
            for k in range(levels):
                acc = jnp.where(lane == k, rolled(tile(name, k), k - c, 1), acc)
            to_y[i] = acc
    for spec, to_x in ((hi_x, to_xp), (lo_x, to_xm)):
        for i, (name, r) in enumerate(spec):
            if only is not None and i != only:
                continue
            for g in range(KPAD // nx):
                acc = zero
                for k in range(g * nx, min(levels, (g + 1) * nx)):
                    acc = jnp.where(row == k % nx, rolled(tile(name, k), k - r, 0), acc)
                to_x[i, g * nx : (g + 1) * nx, :] = acc


def state_tile(winds, thermo):
    refs = {"u": winds.at[0], "v": winds.at[1], "p": thermo.at[0], "th": thermo.at[1], "q": thermo.at[2]}
    return lambda name, k: refs[name][k]


def pack_kernel(tots, winds, thermo, to_xp, to_xm, to_yp, to_ym):
    levels = winds.shape[1]
    pack_halos(levels, state_tile(winds, thermo), to_xp, to_xm, to_yp, to_ym)
    to_xp[0, levels : levels + 1, :] = tots[0:1, :]
    to_xm[0, levels : levels + 1, :] = tots[1:2, :]


def substep_kernel(devices, add_heat, *refs):
    if add_heat:
        profile, winds, thermo, heating = refs[:4]
        refs = refs[4:]
    else:
        winds, thermo = refs[:2]
        refs = refs[2:]
    from_xm, from_xp, from_ym, from_yp, winds_out, thermo_out = refs[:6]
    sends = refs[6:]
    levels, nx, ny = winds.shape[1:]
    ix, iy = lax.axis_index("gx"), lax.axis_index("gy")
    edge = (ix == 0, ix == devices[0] - 1, iy == 0, iy == devices[1] - 1)
    row = lax.broadcasted_iota(jnp.int32, (nx, ny), 0)
    lane = lax.broadcasted_iota(jnp.int32, (nx, ny), 1)
    xm = lambda i, k: rolled(from_xm[i, (k // nx) * nx : (k // nx + 1) * nx, :], -k, 0)
    xp = lambda i, k: rolled(from_xp[i, (k // nx) * nx : (k // nx + 1) * nx, :], nx - 1 - k, 0)
    ym = lambda i, k: rolled(from_ym[i], -k, 1)
    yp = lambda i, k: rolled(from_yp[i], ny - 1 - k, 1)
    x_up = lambda f, h: jnp.where(row == nx - 1, h, pltpu.roll(f, nx - 1, 0))
    x_dn = lambda f, h: jnp.where(row == 0, h, pltpu.roll(f, 1, 0))
    y_up = lambda f, h: jnp.where(lane == ny - 1, h, pltpu.roll(f, ny - 1, 1))
    y_dn = lambda f, h: jnp.where(lane == 0, h, pltpu.roll(f, 1, 1))

    def vert(ref, k):
        upper = ref[k + 1] if k + 1 < levels else jnp.zeros((nx, ny), jnp.float32)
        lower = ref[k - 1] if k > 0 else jnp.zeros((nx, ny), jnp.float32)
        return upper - lower

    press = thermo.at[0]
    for k in range(levels):
        p = press[k]
        theta = thermo[1, k]
        winds_out[0, k] = winds[0, k] - 0.25 * (x_up(p, xp(1, k)) - x_dn(p, xm(1, k)))
        winds_out[1, k] = winds[1, k] - 0.25 * (y_up(p, yp(1, k)) - y_dn(p, ym(1, k)))
        up_n = winds[2, k] - 0.25 * vert(press, k) + 0.1 * theta
        winds_out[2, k] = up_n
        for index in (1, 2):
            field = thermo[index, k]
            east_c = x_up(field, xp(index + 2, k))
            west_c = x_dn(field, xm(index + 2, k))
            lap = east_c + west_c + y_up(field, yp(index + 2, k)) + y_dn(field, ym(index + 2, k)) - 4.0 * field
            new = field + 0.1 * lap - 0.15 * (east_c - west_c)
            if index == 1:
                new = new - 0.1 * up_n
                if add_heat:
                    new = new + profile[k] * heating[...]
            thermo_out[index, k] = new
    up_out = winds_out.at[2]
    for k in range(levels):
        p = press[k]
        east_hi = xp(2, k) - 0.25 * (xp(0, k) - p)
        east_lo = xm(2, k) - 0.25 * (p - xm(0, k))
        north_hi = yp(2, k) - 0.25 * (yp(0, k) - p)
        north_lo = ym(2, k) - 0.25 * (p - ym(0, k))
        east_hi = jnp.where(edge[1], 0.0, east_hi)
        east_lo = jnp.where(edge[0], 0.0, east_lo)
        north_hi = jnp.where(edge[3], 0.0, north_hi)
        north_lo = jnp.where(edge[2], 0.0, north_lo)
        east_n = winds_out[0, k]
        north_n = winds_out[1, k]
        diverge = (x_up(east_n, east_hi) - x_dn(east_n, east_lo)) + (
            y_up(north_n, north_hi) - y_dn(north_n, north_lo)
        )
        thermo_out[0, k] = p - 0.25 * (diverge + vert(up_out, k))
    if sends:
        pack_halos(levels, state_tile(winds_out, thermo_out), *sends)


def halo_shapes(winds):
    _, levels, nx, ny = winds.shape
    x_msg = jax.ShapeDtypeStruct((5, KPAD, ny), jnp.float32)
    y_msg = jax.ShapeDtypeStruct((5, nx, ny), jnp.float32)
    return (x_msg, x_msg, y_msg, y_msg)


VMEM = pl.BlockSpec(memory_space=pltpu.VMEM)


def pack(winds, thermo, tots):
    return pl.pallas_call(
        pack_kernel,
        out_shape=halo_shapes(winds),
        in_specs=[VMEM] * 3,
        out_specs=(VMEM,) * 4,
    )(tots, winds, thermo)


def heat_kernel(profile, heating, thermo, xp_in, xm_in, yp_in, ym_in, thermo_out, to_xp, to_xm, to_yp, to_ym):
    levels = thermo.shape[1]
    for k in range(levels):
        thermo_out[0, k] = thermo[0, k]
        thermo_out[2, k] = thermo[2, k]
        thermo_out[1, k] = thermo[1, k] + profile[k] * heating[...]
    for src, dst in ((xp_in, to_xp), (xm_in, to_xm), (yp_in, to_yp), (ym_in, to_ym)):
        for i in (0, 1, 2, 4):
            dst[i] = src[i]
    refs = {"th": thermo_out.at[1]}
    pack_halos(levels, lambda name, k: refs[name][k], to_xp, to_xm, to_yp, to_ym, only=3)


def add_heat(thermo, sends, profile, heating):
    smem = pl.BlockSpec(memory_space=pltpu.SMEM)
    return pl.pallas_call(
        heat_kernel,
        out_shape=(jax.ShapeDtypeStruct(thermo.shape, jnp.float32),) + tuple(
            jax.ShapeDtypeStruct(m.shape, jnp.float32) for m in sends
        ),
        in_specs=[smem] + [VMEM] * 6,
        out_specs=(VMEM,) * 5,
    )(profile, heating, thermo, *sends)


def substep(winds, thermo, halos, heat, emit):
    outs = (
        jax.ShapeDtypeStruct(winds.shape, jnp.float32),
        jax.ShapeDtypeStruct(thermo.shape, jnp.float32),
    )
    if emit:
        outs = outs + halo_shapes(winds)
    devices = (lax.axis_size("gx"), lax.axis_size("gy"))
    smem = pl.BlockSpec(memory_space=pltpu.SMEM)
    heat_args = (heat[0], winds, thermo, heat[1]) if heat else (winds, thermo)
    heat_specs = [smem, VMEM, VMEM, VMEM] if heat else [VMEM, VMEM]
    return pl.pallas_call(
        functools.partial(substep_kernel, devices, bool(heat)),
        out_shape=outs,
        in_specs=heat_specs + [VMEM] * 4,
        out_specs=(VMEM,) * len(outs),
    )(*heat_args, *halos)


def per_device(winds, thermo, terrain, shadow_len, sector, land_mask):
    cols_x, cols_y = terrain.shape
    levels = winds.shape[1]
    ramp = (ramp_rate * jnp.arange(cols_x).astype(jnp.float32) / cols_x)[:, None]
    west_terms = jnp.exp(terrain + ramp) * (shade_scale / cols_x)
    east_terms = jnp.exp(terrain - ramp) * (shade_scale / cols_x)
    prefix = jnp.cumsum(west_terms, axis=0) - west_terms
    west_tot = jnp.sum(west_terms, axis=0)
    east_tot = jnp.sum(east_terms, axis=0)
    suffix = east_tot[None, :] - jnp.cumsum(east_terms, axis=0)

    to_xp, to_xm, to_yp, to_ym = pack(winds, thermo, jnp.stack([west_tot, east_tot]))
    far = {}
    for step in range(ITERS):
        from_xm = shifted(to_xp, "gx", 1)
        from_xp = shifted(to_xm, "gx", -1)
        from_ym = shifted(to_yp, "gy", 1)
        from_yp = shifted(to_ym, "gy", -1)
        if step == 0:
            near_w = shifted(west_tot, "gx", 2)
            near_e = shifted(east_tot, "gx", -2)
            far[("w", 1)] = from_xm[0, levels]
            far[("e", 1)] = from_xp[0, levels]
            far[("w", 2)] = near_w
            far[("e", 2)] = near_e
            relay_w = shifted(jnp.stack([far[("w", 1)], near_w]), "gx", 2)
            relay_e = shifted(jnp.stack([far[("e", 1)], near_e]), "gx", -2)
            far[("w", 3)], far[("w", 4)] = relay_w[0], relay_w[1]
            far[("e", 3)], far[("e", 4)] = relay_e[0], relay_e[1]
            west_far = jnp.zeros((cols_y,), jnp.float32)
            east_far = jnp.zeros((cols_y,), jnp.float32)
            for reach in range(1, LMAX + 1):
                weight = jnp.where(shadow_len >= reach, math.exp(-decay_rate * reach), 0.0)
                west_far = west_far + weight * far[("w", reach)]
                east_far = east_far + weight * far[("e", reach)]
            west_occ = (prefix + west_far[None, :]) * jnp.exp(-terrain - ramp)
            east_occ = (suffix + east_far[None, :]) * jnp.exp(ramp - terrain)
            sun = jnp.where(sector[None, :] == 0, 1.0 / (1.0 + west_occ), 1.0 / (1.0 + east_occ))
            sky = 1.0 / (1.0 + 0.5 * (west_occ + east_occ))
            land = land_mask[0, 0].astype(jnp.float32)
            heating = land * (0.7 * sun + 0.3 * sky) + (1.0 - land) * 0.3 * sky
            profile = jnp.exp(-jnp.arange(levels).astype(jnp.float32) / 4.0)
        halos = (from_xm, from_xp, from_ym, from_yp)
        emit = step + 1 < ITERS
        outs = substep(winds, thermo, halos, () if step == 0 else (profile, heating), emit)
        winds, thermo = outs[0], outs[1]
        if step == 0:
            thermo, *sends = add_heat(thermo, outs[2:], profile, heating)
        if emit:
            to_xp, to_xm, to_yp, to_ym = sends
    return (winds, thermo)


def solution(mesh):
    return jax.shard_map(
        per_device,
        mesh=mesh,
        in_specs=(
            P(None, None, "gx", "gy"),
            P(None, None, "gx", "gy"),
            P("gx", "gy"),
            P("gy"),
            P("gy"),
            P("gx", "gy"),
        ),
        out_specs=(P(None, None, "gx", "gy"), P(None, None, "gx", "gy")),
        check_vma=False,
    )
```

```python
import functools
import math

import jax
import jax.numpy as jnp
from jax import lax
from jax.experimental import pallas as pl
from jax.experimental.pallas import tpu as pltpu
from jax.sharding import PartitionSpec as P

ITERS = 2
LMAX = 4


ramp_rate = 0.7
decay_rate = 0.25
shade_scale = 0.1


def shifted(block, axis, distance):
    devices = range(lax.axis_size(axis))
    route = [(i, i + distance) for i in devices if i + distance in devices]
    return lax.ppermute(block, axis, route)


def vertical(field):
    zero = jnp.zeros((1,) + field.shape[1:], jnp.float32)
    upper = jnp.concatenate([field[1:], zero], axis=0)
    lower = jnp.concatenate([zero, field[:-1]], axis=0)
    return upper - lower


KPAD = 32


def rolled(a, shift, axis):
    shift %= a.shape[axis]
    return pltpu.roll(a, shift, axis) if shift else a


def pack_halos(levels, tile, to_xp, to_xm, to_yp, to_ym, only=None):
    nx, ny = to_yp.shape[1] // KPAD, to_xp.shape[2]
    row = lax.broadcasted_iota(jnp.int32, (nx, ny), 0)
    hi_x = (("p", nx - 2), ("p", nx - 1), ("u", nx - 1), ("th", nx - 1), ("q", nx - 1))
    lo_x = (("p", 1), ("p", 0), ("u", 0), ("th", 0), ("q", 0))
    hi_y = (("p", ny - 2), ("p", ny - 1), ("v", ny - 1), ("th", ny - 1), ("q", ny - 1))
    lo_y = (("p", 1), ("p", 0), ("v", 0), ("th", 0), ("q", 0))
    zero = jnp.zeros((nx, ny), jnp.float32)
    names = sorted({name for name, _ in hi_y + lo_y if only is None or name == "th"})
    flipped = {}
    for name in names:
        stacked = jnp.concatenate([tile(name, k) for k in range(levels)] + [zero] * (KPAD - levels), axis=0)
        flipped[name] = stacked.T
    for spec, to_y in ((hi_y, to_yp), (lo_y, to_ym)):
        for i, (name, c) in enumerate(spec):
            if only is not None and i != only:
                continue
            to_y[i : i + 1, :] = flipped[name][c : c + 1, :]
        if only is None:
            to_y[len(spec) :, :] = jnp.zeros((to_y.shape[0] - len(spec), to_y.shape[1]), jnp.float32)
    for spec, to_x in ((hi_x, to_xp), (lo_x, to_xm)):
        for i, (name, r) in enumerate(spec):
            if only is not None and i != only:
                continue
            for g in range(KPAD // nx):
                acc = zero
                for k in range(g * nx, min(levels, (g + 1) * nx)):
                    acc = jnp.where(row == k % nx, rolled(tile(name, k), k - r, 0), acc)
                to_x[i, g * nx : (g + 1) * nx, :] = acc


def state_tile(winds, thermo):
    refs = {"u": winds.at[0], "v": winds.at[1], "p": thermo.at[0], "th": thermo.at[1], "q": thermo.at[2]}
    return lambda name, k: refs[name][k]


def pack_kernel(tots, winds, thermo, to_xp, to_xm, to_yp, to_ym):
    levels = winds.shape[1]
    pack_halos(levels, state_tile(winds, thermo), to_xp, to_xm, to_yp, to_ym)
    to_xp[0, levels : levels + 1, :] = tots[0:1, :]
    to_xm[0, levels : levels + 1, :] = tots[1:2, :]


def substep_kernel(devices, add_heat, *refs):
    if add_heat:
        profile, winds, thermo, heating = refs[:4]
        refs = refs[4:]
    else:
        winds, thermo = refs[:2]
        refs = refs[2:]
    from_xm, from_xp, from_ym, from_yp, winds_out, thermo_out = refs[:6]
    sends, y_halo = refs[6:-1], refs[-1]
    levels, nx, ny = winds.shape[1:]
    ix, iy = lax.axis_index("gx"), lax.axis_index("gy")
    edge = (ix == 0, ix == devices[0] - 1, iy == 0, iy == devices[1] - 1)
    row = lax.broadcasted_iota(jnp.int32, (nx, ny), 0)
    lane = lax.broadcasted_iota(jnp.int32, (nx, ny), 1)
    xm = lambda i, k: rolled(from_xm[i, (k // nx) * nx : (k // nx + 1) * nx, :], -k, 0)
    xp = lambda i, k: rolled(from_xp[i, (k // nx) * nx : (k // nx + 1) * nx, :], nx - 1 - k, 0)
    edge_row = lax.broadcasted_iota(jnp.int32, (ny, KPAD * nx), 0)
    for i in range(5):
        lo = jnp.broadcast_to(from_ym[i : i + 1, :], (ny, KPAD * nx))
        hi = jnp.broadcast_to(from_yp[i : i + 1, :], (ny, KPAD * nx))
        y_halo[i] = jnp.where(edge_row == 0, lo, jnp.where(edge_row == ny - 1, hi, 0.0)).T
    yh = lambda i, k: y_halo[i, k * nx : (k + 1) * nx, :]
    x_up = lambda f, h: jnp.where(row == nx - 1, h, pltpu.roll(f, nx - 1, 0))
    x_dn = lambda f, h: jnp.where(row == 0, h, pltpu.roll(f, 1, 0))
    y_up = lambda f, h: jnp.where(lane == ny - 1, h, pltpu.roll(f, ny - 1, 1))
    y_dn = lambda f, h: jnp.where(lane == 0, h, pltpu.roll(f, 1, 1))

    def vert(ref, k):
        upper = ref[k + 1] if k + 1 < levels else jnp.zeros((nx, ny), jnp.float32)
        lower = ref[k - 1] if k > 0 else jnp.zeros((nx, ny), jnp.float32)
        return upper - lower

    press = thermo.at[0]
    for k in range(levels):
        p = press[k]
        theta = thermo[1, k]
        winds_out[0, k] = winds[0, k] - 0.25 * (x_up(p, xp(1, k)) - x_dn(p, xm(1, k)))
        winds_out[1, k] = winds[1, k] - 0.25 * (y_up(p, yh(1, k)) - y_dn(p, yh(1, k)))
        up_n = winds[2, k] - 0.25 * vert(press, k) + 0.1 * theta
        winds_out[2, k] = up_n
        for index in (1, 2):
            field = thermo[index, k]
            east_c = x_up(field, xp(index + 2, k))
            west_c = x_dn(field, xm(index + 2, k))
            lap = east_c + west_c + y_up(field, yh(index + 2, k)) + y_dn(field, yh(index + 2, k)) - 4.0 * field
            new = field + 0.1 * lap - 0.15 * (east_c - west_c)
            if index == 1:
                new = new - 0.1 * up_n
                if add_heat:
                    new = new + profile[k] * heating[...]
            thermo_out[index, k] = new
    up_out = winds_out.at[2]
    for k in range(levels):
        p = press[k]
        east_hi = xp(2, k) - 0.25 * (xp(0, k) - p)
        east_lo = xm(2, k) - 0.25 * (p - xm(0, k))
        north_hi = yh(2, k) - 0.25 * (yh(0, k) - p)
        north_lo = yh(2, k) - 0.25 * (p - yh(0, k))
        east_hi = jnp.where(edge[1], 0.0, east_hi)
        east_lo = jnp.where(edge[0], 0.0, east_lo)
        north_hi = jnp.where(edge[3], 0.0, north_hi)
        north_lo = jnp.where(edge[2], 0.0, north_lo)
        east_n = winds_out[0, k]
        north_n = winds_out[1, k]
        diverge = (x_up(east_n, east_hi) - x_dn(east_n, east_lo)) + (
            y_up(north_n, north_hi) - y_dn(north_n, north_lo)
        )
        thermo_out[0, k] = p - 0.25 * (diverge + vert(up_out, k))
    if sends:
        pack_halos(levels, state_tile(winds_out, thermo_out), *sends)


def halo_shapes(winds):
    _, levels, nx, ny = winds.shape
    x_msg = jax.ShapeDtypeStruct((5, KPAD, ny), jnp.float32)
    y_msg = jax.ShapeDtypeStruct((8, KPAD * nx), jnp.float32)
    return (x_msg, x_msg, y_msg, y_msg)


VMEM = pl.BlockSpec(memory_space=pltpu.VMEM)


def pack(winds, thermo, tots):
    return pl.pallas_call(
        pack_kernel,
        out_shape=halo_shapes(winds),
        in_specs=[VMEM] * 3,
        out_specs=(VMEM,) * 4,
    )(tots, winds, thermo)


def heat_kernel(profile, heating, thermo, xp_in, xm_in, yp_in, ym_in, thermo_out, to_xp, to_xm, to_yp, to_ym):
    levels = thermo.shape[1]
    for k in range(levels):
        thermo_out[0, k] = thermo[0, k]
        thermo_out[2, k] = thermo[2, k]
        thermo_out[1, k] = thermo[1, k] + profile[k] * heating[...]
    for src, dst in ((xp_in, to_xp), (xm_in, to_xm), (yp_in, to_yp), (ym_in, to_ym)):
        for i in range(src.shape[0]):
            if i != 3:
                dst[i] = src[i]
    refs = {"th": thermo_out.at[1]}
    pack_halos(levels, lambda name, k: refs[name][k], to_xp, to_xm, to_yp, to_ym, only=3)


def add_heat(thermo, sends, profile, heating):
    smem = pl.BlockSpec(memory_space=pltpu.SMEM)
    return pl.pallas_call(
        heat_kernel,
        out_shape=(jax.ShapeDtypeStruct(thermo.shape, jnp.float32),) + tuple(
            jax.ShapeDtypeStruct(m.shape, jnp.float32) for m in sends
        ),
        in_specs=[smem] + [VMEM] * 6,
        out_specs=(VMEM,) * 5,
    )(profile, heating, thermo, *sends)


def substep(winds, thermo, halos, heat, emit):
    outs = (
        jax.ShapeDtypeStruct(winds.shape, jnp.float32),
        jax.ShapeDtypeStruct(thermo.shape, jnp.float32),
    )
    if emit:
        outs = outs + halo_shapes(winds)
    devices = (lax.axis_size("gx"), lax.axis_size("gy"))
    smem = pl.BlockSpec(memory_space=pltpu.SMEM)
    heat_args = (heat[0], winds, thermo, heat[1]) if heat else (winds, thermo)
    heat_specs = [smem, VMEM, VMEM, VMEM] if heat else [VMEM, VMEM]
    return pl.pallas_call(
        functools.partial(substep_kernel, devices, bool(heat)),
        out_shape=outs,
        in_specs=heat_specs + [VMEM] * 4,
        out_specs=(VMEM,) * len(outs),
        scratch_shapes=[pltpu.VMEM((5, KPAD * winds.shape[2], winds.shape[3]), jnp.float32)],
    )(*heat_args, *halos)


def per_device(winds, thermo, terrain, shadow_len, sector, land_mask):
    cols_x, cols_y = terrain.shape
    levels = winds.shape[1]
    ramp = (ramp_rate * jnp.arange(cols_x).astype(jnp.float32) / cols_x)[:, None]
    west_terms = jnp.exp(terrain + ramp) * (shade_scale / cols_x)
    east_terms = jnp.exp(terrain - ramp) * (shade_scale / cols_x)
    prefix = jnp.cumsum(west_terms, axis=0) - west_terms
    west_tot = jnp.sum(west_terms, axis=0)
    east_tot = jnp.sum(east_terms, axis=0)
    suffix = east_tot[None, :] - jnp.cumsum(east_terms, axis=0)

    to_xp, to_xm, to_yp, to_ym = pack(winds, thermo, jnp.stack([west_tot, east_tot]))
    far = {}
    for step in range(ITERS):
        from_xm = shifted(to_xp, "gx", 1)
        from_xp = shifted(to_xm, "gx", -1)
        from_ym = shifted(to_yp, "gy", 1)
        from_yp = shifted(to_ym, "gy", -1)
        if step == 0:
            near_w = shifted(west_tot, "gx", 2)
            near_e = shifted(east_tot, "gx", -2)
            far[("w", 1)] = from_xm[0, levels]
            far[("e", 1)] = from_xp[0, levels]
            far[("w", 2)] = near_w
            far[("e", 2)] = near_e
            relay_w = shifted(jnp.stack([far[("w", 1)], near_w]), "gx", 2)
            relay_e = shifted(jnp.stack([far[("e", 1)], near_e]), "gx", -2)
            far[("w", 3)], far[("w", 4)] = relay_w[0], relay_w[1]
            far[("e", 3)], far[("e", 4)] = relay_e[0], relay_e[1]
            west_far = jnp.zeros((cols_y,), jnp.float32)
            east_far = jnp.zeros((cols_y,), jnp.float32)
            for reach in range(1, LMAX + 1):
                weight = jnp.where(shadow_len >= reach, math.exp(-decay_rate * reach), 0.0)
                west_far = west_far + weight * far[("w", reach)]
                east_far = east_far + weight * far[("e", reach)]
            west_occ = (prefix + west_far[None, :]) * jnp.exp(-terrain - ramp)
            east_occ = (suffix + east_far[None, :]) * jnp.exp(ramp - terrain)
            sun = jnp.where(sector[None, :] == 0, 1.0 / (1.0 + west_occ), 1.0 / (1.0 + east_occ))
            sky = 1.0 / (1.0 + 0.5 * (west_occ + east_occ))
            land = land_mask[0, 0].astype(jnp.float32)
            heating = land * (0.7 * sun + 0.3 * sky) + (1.0 - land) * 0.3 * sky
            profile = jnp.exp(-jnp.arange(levels).astype(jnp.float32) / 4.0)
        halos = (from_xm, from_xp, from_ym, from_yp)
        emit = step + 1 < ITERS
        outs = substep(winds, thermo, halos, () if step == 0 else (profile, heating), emit)
        winds, thermo = outs[0], outs[1]
        if step == 0:
            thermo, *sends = add_heat(thermo, outs[2:], profile, heating)
        if emit:
            to_xp, to_xm, to_yp, to_ym = sends
    return (winds, thermo)


def solution(mesh):
    return jax.shard_map(
        per_device,
        mesh=mesh,
        in_specs=(
            P(None, None, "gx", "gy"),
            P(None, None, "gx", "gy"),
            P("gx", "gy"),
            P("gy"),
            P("gy"),
            P("gx", "gy"),
        ),
        out_specs=(P(None, None, "gx", "gy"), P(None, None, "gx", "gy")),
        check_vma=False,
    )
```

```python
import functools
import math

import jax
import jax.numpy as jnp
from jax import lax
from jax.experimental import pallas as pl
from jax.experimental.pallas import tpu as pltpu
from jax.sharding import PartitionSpec as P

ITERS = 2
LMAX = 4


ramp_rate = 0.7
decay_rate = 0.25
shade_scale = 0.1


def shifted(block, axis, distance):
    devices = range(lax.axis_size(axis))
    route = [(i, i + distance) for i in devices if i + distance in devices]
    return lax.ppermute(block, axis, route)


def vertical(field):
    zero = jnp.zeros((1,) + field.shape[1:], jnp.float32)
    upper = jnp.concatenate([field[1:], zero], axis=0)
    lower = jnp.concatenate([zero, field[:-1]], axis=0)
    return upper - lower


KPAD = 32


def rolled(a, shift, axis):
    shift %= a.shape[axis]
    return pltpu.roll(a, shift, axis) if shift else a


def pack_halos(levels, tile, to_xp, to_xm, to_yp, to_ym, only=None):
    nx, ny = to_yp.shape[1] // KPAD, to_xp.shape[2]
    row = lax.broadcasted_iota(jnp.int32, (nx, ny), 0)
    hi_x = (("p", nx - 2), ("p", nx - 1), ("u", nx - 1), ("th", nx - 1), ("q", nx - 1))
    lo_x = (("p", 1), ("p", 0), ("u", 0), ("th", 0), ("q", 0))
    hi_y = (("p", ny - 2), ("p", ny - 1), ("v", ny - 1), ("th", ny - 1), ("q", ny - 1))
    lo_y = (("p", 1), ("p", 0), ("v", 0), ("th", 0), ("q", 0))
    zero = jnp.zeros((nx, ny), jnp.float32)
    names = sorted({name for name, _ in hi_y + lo_y if only is None or name == "th"})
    flipped = {}
    for name in names:
        stacked = jnp.concatenate([tile(name, k) for k in range(levels)] + [zero] * (KPAD - levels), axis=0)
        flipped[name] = stacked.T
    for spec, to_y in ((hi_y, to_yp), (lo_y, to_ym)):
        for i, (name, c) in enumerate(spec):
            if only is not None and i != only:
                continue
            to_y[i : i + 1, :] = flipped[name][c : c + 1, :]
        if only is None:
            to_y[len(spec) :, :] = jnp.zeros((to_y.shape[0] - len(spec), to_y.shape[1]), jnp.float32)
    for spec, to_x in ((hi_x, to_xp), (lo_x, to_xm)):
        for i, (name, r) in enumerate(spec):
            if only is not None and i != only:
                continue
            for g in range(KPAD // nx):
                acc = zero
                for k in range(g * nx, min(levels, (g + 1) * nx)):
                    acc = jnp.where(row == k % nx, rolled(tile(name, k), k - r, 0), acc)
                to_x[i, g * nx : (g + 1) * nx, :] = acc


def state_tile(winds, thermo):
    refs = {"u": winds.at[0], "v": winds.at[1], "p": thermo.at[0], "th": thermo.at[1], "q": thermo.at[2]}
    return lambda name, k: refs[name][k]


def pack_kernel(tots, winds, thermo, to_xp, to_xm, to_yp, to_ym):
    levels = winds.shape[1]
    pack_halos(levels, state_tile(winds, thermo), to_xp, to_xm, to_yp, to_ym)
    to_xp[0, levels : levels + 1, :] = tots[0:1, :]
    to_xm[0, levels : levels + 1, :] = tots[1:2, :]


def substep_kernel(devices, add_heat, *refs):
    if add_heat:
        profile, winds, thermo, heating = refs[:4]
        refs = refs[4:]
    else:
        winds, thermo = refs[:2]
        refs = refs[2:]
    from_xm, from_xp, from_ym, from_yp, winds_out, thermo_out = refs[:6]
    sends, y_halo = refs[6:-1], refs[-1]
    levels, nx, ny = winds.shape[1:]
    ix, iy = lax.axis_index("gx"), lax.axis_index("gy")
    edge = (ix == 0, ix == devices[0] - 1, iy == 0, iy == devices[1] - 1)
    row = lax.broadcasted_iota(jnp.int32, (nx, ny), 0)
    lane = lax.broadcasted_iota(jnp.int32, (nx, ny), 1)
    xm = lambda i, k: rolled(from_xm[i, (k // nx) * nx : (k // nx + 1) * nx, :], -k, 0)
    xp = lambda i, k: rolled(from_xp[i, (k // nx) * nx : (k // nx + 1) * nx, :], nx - 1 - k, 0)
    edge_row = lax.broadcasted_iota(jnp.int32, (ny, KPAD * nx), 0)
    for i in range(5):
        lo = jnp.broadcast_to(from_ym[i : i + 1, :], (ny, KPAD * nx))
        hi = jnp.broadcast_to(from_yp[i : i + 1, :], (ny, KPAD * nx))
        y_halo[i] = jnp.where(edge_row == 0, lo, jnp.where(edge_row == ny - 1, hi, 0.0)).T
    yh = lambda i, k: y_halo[i, k * nx : (k + 1) * nx, :]
    x_up = lambda f, h: jnp.where(row == nx - 1, h, pltpu.roll(f, nx - 1, 0))
    x_dn = lambda f, h: jnp.where(row == 0, h, pltpu.roll(f, 1, 0))
    y_up = lambda f, h: jnp.where(lane == ny - 1, h, pltpu.roll(f, ny - 1, 1))
    y_dn = lambda f, h: jnp.where(lane == 0, h, pltpu.roll(f, 1, 1))

    def vert(ref, k):
        upper = ref[k + 1] if k + 1 < levels else jnp.zeros((nx, ny), jnp.float32)
        lower = ref[k - 1] if k > 0 else jnp.zeros((nx, ny), jnp.float32)
        return upper - lower

    press = thermo.at[0]
    for k in range(levels):
        p = press[k]
        theta = thermo[1, k]
        winds_out[0, k] = winds[0, k] - 0.25 * (x_up(p, xp(1, k)) - x_dn(p, xm(1, k)))
        winds_out[1, k] = winds[1, k] - 0.25 * (y_up(p, yh(1, k)) - y_dn(p, yh(1, k)))
        up_n = winds[2, k] - 0.25 * vert(press, k) + 0.1 * theta
        winds_out[2, k] = up_n
        for index in (1, 2):
            field = thermo[index, k]
            east_c = x_up(field, xp(index + 2, k))
            west_c = x_dn(field, xm(index + 2, k))
            lap = east_c + west_c + y_up(field, yh(index + 2, k)) + y_dn(field, yh(index + 2, k)) - 4.0 * field
            new = field + 0.1 * lap - 0.15 * (east_c - west_c)
            if index == 1:
                new = new - 0.1 * up_n
                if add_heat:
                    new = new + profile[k] * heating[...]
            thermo_out[index, k] = new
    up_out = winds_out.at[2]
    for k in range(levels):
        p = press[k]
        east_hi = xp(2, k) - 0.25 * (xp(0, k) - p)
        east_lo = xm(2, k) - 0.25 * (p - xm(0, k))
        north_hi = yh(2, k) - 0.25 * (yh(0, k) - p)
        north_lo = yh(2, k) - 0.25 * (p - yh(0, k))
        east_hi = jnp.where(edge[1], 0.0, east_hi)
        east_lo = jnp.where(edge[0], 0.0, east_lo)
        north_hi = jnp.where(edge[3], 0.0, north_hi)
        north_lo = jnp.where(edge[2], 0.0, north_lo)
        east_n = winds_out[0, k]
        north_n = winds_out[1, k]
        diverge = (x_up(east_n, east_hi) - x_dn(east_n, east_lo)) + (
            y_up(north_n, north_hi) - y_dn(north_n, north_lo)
        )
        thermo_out[0, k] = p - 0.25 * (diverge + vert(up_out, k))
    if sends:
        pack_halos(levels, state_tile(winds_out, thermo_out), *sends)


def halo_shapes(winds):
    _, levels, nx, ny = winds.shape
    x_msg = jax.ShapeDtypeStruct((5, KPAD, ny), jnp.float32)
    y_msg = jax.ShapeDtypeStruct((8, KPAD * nx), jnp.float32)
    return (x_msg, x_msg, y_msg, y_msg)


VMEM = pl.BlockSpec(memory_space=pltpu.VMEM)


def pack(winds, thermo, tots):
    return pl.pallas_call(
        pack_kernel,
        out_shape=halo_shapes(winds),
        in_specs=[VMEM] * 3,
        out_specs=(VMEM,) * 4,
    )(tots, winds, thermo)


def heat_kernel(profile, heating, thermo, xp_in, xm_in, yp_in, ym_in, thermo_out, to_xp, to_xm, to_yp, to_ym):
    levels = thermo.shape[1]
    for k in range(levels):
        thermo_out[0, k] = thermo[0, k]
        thermo_out[2, k] = thermo[2, k]
        thermo_out[1, k] = thermo[1, k] + profile[k] * heating[...]
    for src, dst in ((xp_in, to_xp), (xm_in, to_xm), (yp_in, to_yp), (ym_in, to_ym)):
        for i in range(src.shape[0]):
            if i != 3:
                dst[i] = src[i]
    refs = {"th": thermo_out.at[1]}
    pack_halos(levels, lambda name, k: refs[name][k], to_xp, to_xm, to_yp, to_ym, only=3)


def add_heat(thermo, sends, profile, heating):
    smem = pl.BlockSpec(memory_space=pltpu.SMEM)
    return pl.pallas_call(
        heat_kernel,
        out_shape=(jax.ShapeDtypeStruct(thermo.shape, jnp.float32),) + tuple(
            jax.ShapeDtypeStruct(m.shape, jnp.float32) for m in sends
        ),
        in_specs=[smem] + [VMEM] * 6,
        out_specs=(VMEM,) * 5,
    )(profile, heating, thermo, *sends)


def substep(winds, thermo, halos, heat, emit):
    outs = (
        jax.ShapeDtypeStruct(winds.shape, jnp.float32),
        jax.ShapeDtypeStruct(thermo.shape, jnp.float32),
    )
    if emit:
        outs = outs + halo_shapes(winds)
    devices = (lax.axis_size("gx"), lax.axis_size("gy"))
    smem = pl.BlockSpec(memory_space=pltpu.SMEM)
    heat_args = (heat[0], winds, thermo, heat[1]) if heat else (winds, thermo)
    heat_specs = [smem, VMEM, VMEM, VMEM] if heat else [VMEM, VMEM]
    return pl.pallas_call(
        functools.partial(substep_kernel, devices, bool(heat)),
        out_shape=outs,
        in_specs=heat_specs + [VMEM] * 4,
        out_specs=(VMEM,) * len(outs),
        scratch_shapes=[pltpu.VMEM((5, KPAD * winds.shape[2], winds.shape[3]), jnp.float32)],
    )(*heat_args, *halos)


def per_device(winds, thermo, terrain, shadow_len, sector, land_mask):
    cols_x, cols_y = terrain.shape
    levels = winds.shape[1]
    ramp = (ramp_rate * jnp.arange(cols_x).astype(jnp.float32) / cols_x)[:, None]
    west_terms = jnp.exp(terrain + ramp) * (shade_scale / cols_x)
    east_terms = jnp.exp(terrain - ramp) * (shade_scale / cols_x)
    prefix = jnp.cumsum(west_terms, axis=0) - west_terms
    west_tot = jnp.sum(west_terms, axis=0)
    east_tot = jnp.sum(east_terms, axis=0)
    suffix = east_tot[None, :] - jnp.cumsum(east_terms, axis=0)

    to_xp, to_xm, to_yp, to_ym = pack(winds, thermo, jnp.stack([west_tot, east_tot]))
    far = {}
    for step in range(ITERS):
        from_xm = shifted(to_xp, "gx", 1)
        from_xp = shifted(to_xm, "gx", -1)
        from_ym = shifted(to_yp, "gy", 1)
        from_yp = shifted(to_ym, "gy", -1)
        if step == 0:
            near_w = shifted(to_xp[0, levels], "gx", 2)
            near_e = shifted(to_xm[0, levels], "gx", -2)
            far[("w", 1)] = from_xm[0, levels]
            far[("e", 1)] = from_xp[0, levels]
            far[("w", 2)] = near_w
            far[("e", 2)] = near_e
            relay_w = shifted(jnp.stack([far[("w", 1)], near_w]), "gx", 2)
            relay_e = shifted(jnp.stack([far[("e", 1)], near_e]), "gx", -2)
            far[("w", 3)], far[("w", 4)] = relay_w[0], relay_w[1]
            far[("e", 3)], far[("e", 4)] = relay_e[0], relay_e[1]
            west_far = jnp.zeros((cols_y,), jnp.float32)
            east_far = jnp.zeros((cols_y,), jnp.float32)
            for reach in range(1, LMAX + 1):
                weight = jnp.where(shadow_len >= reach, math.exp(-decay_rate * reach), 0.0)
                west_far = west_far + weight * far[("w", reach)]
                east_far = east_far + weight * far[("e", reach)]
            west_occ = (prefix + west_far[None, :]) * jnp.exp(-terrain - ramp)
            east_occ = (suffix + east_far[None, :]) * jnp.exp(ramp - terrain)
            sun = jnp.where(sector[None, :] == 0, 1.0 / (1.0 + west_occ), 1.0 / (1.0 + east_occ))
            sky = 1.0 / (1.0 + 0.5 * (west_occ + east_occ))
            land = land_mask[0, 0].astype(jnp.float32)
            heating = land * (0.7 * sun + 0.3 * sky) + (1.0 - land) * 0.3 * sky
            profile = jnp.exp(-jnp.arange(levels).astype(jnp.float32) / 4.0)
        halos = (from_xm, from_xp, from_ym, from_yp)
        emit = step + 1 < ITERS
        outs = substep(winds, thermo, halos, () if step == 0 else (profile, heating), emit)
        winds, thermo = outs[0], outs[1]
        if step == 0:
            thermo, *sends = add_heat(thermo, outs[2:], profile, heating)
        if emit:
            to_xp, to_xm, to_yp, to_ym = sends
    return (winds, thermo)


def solution(mesh):
    return jax.shard_map(
        per_device,
        mesh=mesh,
        in_specs=(
            P(None, None, "gx", "gy"),
            P(None, None, "gx", "gy"),
            P("gx", "gy"),
            P("gy"),
            P("gy"),
            P("gx", "gy"),
        ),
        out_specs=(P(None, None, "gx", "gy"), P(None, None, "gx", "gy")),
        check_vma=False,
    )
```

```python
import functools
import math

import jax
import jax.numpy as jnp
from jax import lax
from jax.experimental import pallas as pl
from jax.experimental.pallas import tpu as pltpu
from jax.sharding import PartitionSpec as P

ITERS = 2
LMAX = 4


ramp_rate = 0.7
decay_rate = 0.25
shade_scale = 0.1


def shifted(block, axis, distance):
    devices = range(lax.axis_size(axis))
    route = [(i, i + distance) for i in devices if i + distance in devices]
    return lax.ppermute(block, axis, route)


def vertical(field):
    zero = jnp.zeros((1,) + field.shape[1:], jnp.float32)
    upper = jnp.concatenate([field[1:], zero], axis=0)
    lower = jnp.concatenate([zero, field[:-1]], axis=0)
    return upper - lower


KPAD = 32


def rolled(a, shift, axis):
    shift %= a.shape[axis]
    return pltpu.roll(a, shift, axis) if shift else a


def pack_halos(levels, tile, to_xp, to_xm, to_yp, to_ym, only=None):
    nx, ny = to_yp.shape[1] // KPAD, to_xp.shape[2]
    row = lax.broadcasted_iota(jnp.int32, (nx, ny), 0)
    hi_x = (("p", nx - 2), ("p", nx - 1), ("u", nx - 1), ("th", nx - 1), ("q", nx - 1))
    lo_x = (("p", 1), ("p", 0), ("u", 0), ("th", 0), ("q", 0))
    hi_y = (("p", ny - 2), ("p", ny - 1), ("v", ny - 1), ("th", ny - 1), ("q", ny - 1))
    lo_y = (("p", 1), ("p", 0), ("v", 0), ("th", 0), ("q", 0))
    zero = jnp.zeros((nx, ny), jnp.float32)
    names = sorted({name for name, _ in hi_y + lo_y if only is None or name == "th"})
    flipped = {}
    for name in names:
        stacked = jnp.concatenate([tile(name, k) for k in range(levels)] + [zero] * (KPAD - levels), axis=0)
        flipped[name] = stacked.T
    for spec, to_y in ((hi_y, to_yp), (lo_y, to_ym)):
        for i, (name, c) in enumerate(spec):
            if only is not None and i != only:
                continue
            to_y[i : i + 1, :] = flipped[name][c : c + 1, :]
        if only is None:
            to_y[len(spec) :, :] = jnp.zeros((to_y.shape[0] - len(spec), to_y.shape[1]), jnp.float32)
    for spec, to_x in ((hi_x, to_xp), (lo_x, to_xm)):
        for i, (name, r) in enumerate(spec):
            if only is not None and i != only:
                continue
            for g in range(KPAD // nx):
                acc = zero
                for k in range(g * nx, min(levels, (g + 1) * nx)):
                    acc = jnp.where(row == k % nx, rolled(tile(name, k), k - r, 0), acc)
                to_x[i, g * nx : (g + 1) * nx, :] = acc


def state_tile(winds, thermo):
    refs = {"u": winds.at[0], "v": winds.at[1], "p": thermo.at[0], "th": thermo.at[1], "q": thermo.at[2]}
    return lambda name, k: refs[name][k]


def pack_kernel(terrain, winds, thermo, to_xp, to_xm, to_yp, to_ym):
    levels, nx = winds.shape[1], winds.shape[2]
    pack_halos(levels, state_tile(winds, thermo), to_xp, to_xm, to_yp, to_ym)
    ramp = ramp_rate * lax.broadcasted_iota(jnp.int32, terrain.shape, 0).astype(jnp.float32) / nx
    height = terrain[...]
    west = jnp.sum(jnp.exp(height + ramp) * (shade_scale / nx), axis=0, keepdims=True)
    east = jnp.sum(jnp.exp(height - ramp) * (shade_scale / nx), axis=0, keepdims=True)
    to_xp[0, levels : levels + 1, :] = west
    to_xm[0, levels : levels + 1, :] = east


def substep_kernel(devices, add_heat, *refs):
    if add_heat:
        profile, winds, thermo, heating = refs[:4]
        refs = refs[4:]
    else:
        winds, thermo = refs[:2]
        refs = refs[2:]
    from_xm, from_xp, from_ym, from_yp, winds_out, thermo_out = refs[:6]
    sends, y_halo = refs[6:-1], refs[-1]
    levels, nx, ny = winds.shape[1:]
    ix, iy = lax.axis_index("gx"), lax.axis_index("gy")
    edge = (ix == 0, ix == devices[0] - 1, iy == 0, iy == devices[1] - 1)
    row = lax.broadcasted_iota(jnp.int32, (nx, ny), 0)
    lane = lax.broadcasted_iota(jnp.int32, (nx, ny), 1)
    xm = lambda i, k: rolled(from_xm[i, (k // nx) * nx : (k // nx + 1) * nx, :], -k, 0)
    xp = lambda i, k: rolled(from_xp[i, (k // nx) * nx : (k // nx + 1) * nx, :], nx - 1 - k, 0)
    edge_row = lax.broadcasted_iota(jnp.int32, (ny, KPAD * nx), 0)
    for i in range(5):
        lo = jnp.broadcast_to(from_ym[i : i + 1, :], (ny, KPAD * nx))
        hi = jnp.broadcast_to(from_yp[i : i + 1, :], (ny, KPAD * nx))
        y_halo[i] = jnp.where(edge_row == 0, lo, jnp.where(edge_row == ny - 1, hi, 0.0)).T
    yh = lambda i, k: y_halo[i, k * nx : (k + 1) * nx, :]
    x_up = lambda f, h: jnp.where(row == nx - 1, h, pltpu.roll(f, nx - 1, 0))
    x_dn = lambda f, h: jnp.where(row == 0, h, pltpu.roll(f, 1, 0))
    y_up = lambda f, h: jnp.where(lane == ny - 1, h, pltpu.roll(f, ny - 1, 1))
    y_dn = lambda f, h: jnp.where(lane == 0, h, pltpu.roll(f, 1, 1))

    def vert(ref, k):
        upper = ref[k + 1] if k + 1 < levels else jnp.zeros((nx, ny), jnp.float32)
        lower = ref[k - 1] if k > 0 else jnp.zeros((nx, ny), jnp.float32)
        return upper - lower

    press = thermo.at[0]
    for k in range(levels):
        p = press[k]
        theta = thermo[1, k]
        winds_out[0, k] = winds[0, k] - 0.25 * (x_up(p, xp(1, k)) - x_dn(p, xm(1, k)))
        winds_out[1, k] = winds[1, k] - 0.25 * (y_up(p, yh(1, k)) - y_dn(p, yh(1, k)))
        up_n = winds[2, k] - 0.25 * vert(press, k) + 0.1 * theta
        winds_out[2, k] = up_n
        for index in (1, 2):
            field = thermo[index, k]
            east_c = x_up(field, xp(index + 2, k))
            west_c = x_dn(field, xm(index + 2, k))
            lap = east_c + west_c + y_up(field, yh(index + 2, k)) + y_dn(field, yh(index + 2, k)) - 4.0 * field
            new = field + 0.1 * lap - 0.15 * (east_c - west_c)
            if index == 1:
                new = new - 0.1 * up_n
                if add_heat:
                    new = new + profile[k] * heating[...]
            thermo_out[index, k] = new
    up_out = winds_out.at[2]
    for k in range(levels):
        p = press[k]
        east_hi = xp(2, k) - 0.25 * (xp(0, k) - p)
        east_lo = xm(2, k) - 0.25 * (p - xm(0, k))
        north_hi = yh(2, k) - 0.25 * (yh(0, k) - p)
        north_lo = yh(2, k) - 0.25 * (p - yh(0, k))
        east_hi = jnp.where(edge[1], 0.0, east_hi)
        east_lo = jnp.where(edge[0], 0.0, east_lo)
        north_hi = jnp.where(edge[3], 0.0, north_hi)
        north_lo = jnp.where(edge[2], 0.0, north_lo)
        east_n = winds_out[0, k]
        north_n = winds_out[1, k]
        diverge = (x_up(east_n, east_hi) - x_dn(east_n, east_lo)) + (
            y_up(north_n, north_hi) - y_dn(north_n, north_lo)
        )
        thermo_out[0, k] = p - 0.25 * (diverge + vert(up_out, k))
    if sends:
        pack_halos(levels, state_tile(winds_out, thermo_out), *sends)


def halo_shapes(winds):
    _, levels, nx, ny = winds.shape
    x_msg = jax.ShapeDtypeStruct((5, KPAD, ny), jnp.float32)
    y_msg = jax.ShapeDtypeStruct((8, KPAD * nx), jnp.float32)
    return (x_msg, x_msg, y_msg, y_msg)


VMEM = pl.BlockSpec(memory_space=pltpu.VMEM)


def pack(winds, thermo, tots):
    return pl.pallas_call(
        pack_kernel,
        out_shape=halo_shapes(winds),
        in_specs=[VMEM] * 3,
        out_specs=(VMEM,) * 4,
    )(tots, winds, thermo)


def heat_kernel(profile, heating, thermo, xp_in, xm_in, yp_in, ym_in, thermo_out, to_xp, to_xm, to_yp, to_ym):
    levels = thermo.shape[1]
    for k in range(levels):
        thermo_out[0, k] = thermo[0, k]
        thermo_out[2, k] = thermo[2, k]
        thermo_out[1, k] = thermo[1, k] + profile[k] * heating[...]
    for src, dst in ((xp_in, to_xp), (xm_in, to_xm), (yp_in, to_yp), (ym_in, to_ym)):
        for i in range(src.shape[0]):
            if i != 3:
                dst[i] = src[i]
    refs = {"th": thermo_out.at[1]}
    pack_halos(levels, lambda name, k: refs[name][k], to_xp, to_xm, to_yp, to_ym, only=3)


def add_heat(thermo, sends, profile, heating):
    smem = pl.BlockSpec(memory_space=pltpu.SMEM)
    return pl.pallas_call(
        heat_kernel,
        out_shape=(jax.ShapeDtypeStruct(thermo.shape, jnp.float32),) + tuple(
            jax.ShapeDtypeStruct(m.shape, jnp.float32) for m in sends
        ),
        in_specs=[smem] + [VMEM] * 6,
        out_specs=(VMEM,) * 5,
    )(profile, heating, thermo, *sends)


def substep(winds, thermo, halos, heat, emit):
    outs = (
        jax.ShapeDtypeStruct(winds.shape, jnp.float32),
        jax.ShapeDtypeStruct(thermo.shape, jnp.float32),
    )
    if emit:
        outs = outs + halo_shapes(winds)
    devices = (lax.axis_size("gx"), lax.axis_size("gy"))
    smem = pl.BlockSpec(memory_space=pltpu.SMEM)
    heat_args = (heat[0], winds, thermo, heat[1]) if heat else (winds, thermo)
    heat_specs = [smem, VMEM, VMEM, VMEM] if heat else [VMEM, VMEM]
    return pl.pallas_call(
        functools.partial(substep_kernel, devices, bool(heat)),
        out_shape=outs,
        in_specs=heat_specs + [VMEM] * 4,
        out_specs=(VMEM,) * len(outs),
        scratch_shapes=[pltpu.VMEM((5, KPAD * winds.shape[2], winds.shape[3]), jnp.float32)],
    )(*heat_args, *halos)


def per_device(winds, thermo, terrain, shadow_len, sector, land_mask):
    cols_x, cols_y = terrain.shape
    levels = winds.shape[1]
    ramp = (ramp_rate * jnp.arange(cols_x).astype(jnp.float32) / cols_x)[:, None]
    west_terms = jnp.exp(terrain + ramp) * (shade_scale / cols_x)
    east_terms = jnp.exp(terrain - ramp) * (shade_scale / cols_x)
    prefix = jnp.cumsum(west_terms, axis=0) - west_terms
    east_tot = jnp.sum(east_terms, axis=0)
    suffix = east_tot[None, :] - jnp.cumsum(east_terms, axis=0)

    to_xp, to_xm, to_yp, to_ym = pack(winds, thermo, terrain)
    far = {}
    for step in range(ITERS):
        from_xm = shifted(to_xp, "gx", 1)
        from_xp = shifted(to_xm, "gx", -1)
        from_ym = shifted(to_yp, "gy", 1)
        from_yp = shifted(to_ym, "gy", -1)
        if step == 0:
            near_w = shifted(to_xp[0, levels], "gx", 2)
            near_e = shifted(to_xm[0, levels], "gx", -2)
            far[("w", 1)] = from_xm[0, levels]
            far[("e", 1)] = from_xp[0, levels]
            far[("w", 2)] = near_w
            far[("e", 2)] = near_e
            relay_w = shifted(jnp.stack([far[("w", 1)], near_w]), "gx", 2)
            relay_e = shifted(jnp.stack([far[("e", 1)], near_e]), "gx", -2)
            far[("w", 3)], far[("w", 4)] = relay_w[0], relay_w[1]
            far[("e", 3)], far[("e", 4)] = relay_e[0], relay_e[1]
            west_far = jnp.zeros((cols_y,), jnp.float32)
            east_far = jnp.zeros((cols_y,), jnp.float32)
            for reach in range(1, LMAX + 1):
                weight = jnp.where(shadow_len >= reach, math.exp(-decay_rate * reach), 0.0)
                west_far = west_far + weight * far[("w", reach)]
                east_far = east_far + weight * far[("e", reach)]
            west_occ = (prefix + west_far[None, :]) * jnp.exp(-terrain - ramp)
            east_occ = (suffix + east_far[None, :]) * jnp.exp(ramp - terrain)
            sun = jnp.where(sector[None, :] == 0, 1.0 / (1.0 + west_occ), 1.0 / (1.0 + east_occ))
            sky = 1.0 / (1.0 + 0.5 * (west_occ + east_occ))
            land = land_mask[0, 0].astype(jnp.float32)
            heating = land * (0.7 * sun + 0.3 * sky) + (1.0 - land) * 0.3 * sky
            profile = jnp.exp(-jnp.arange(levels).astype(jnp.float32) / 4.0)
        halos = (from_xm, from_xp, from_ym, from_yp)
        emit = step + 1 < ITERS
        outs = substep(winds, thermo, halos, () if step == 0 else (profile, heating), emit)
        winds, thermo = outs[0], outs[1]
        if step == 0:
            thermo, *sends = add_heat(thermo, outs[2:], profile, heating)
        if emit:
            to_xp, to_xm, to_yp, to_ym = sends
    return (winds, thermo)


def solution(mesh):
    return jax.shard_map(
        per_device,
        mesh=mesh,
        in_specs=(
            P(None, None, "gx", "gy"),
            P(None, None, "gx", "gy"),
            P("gx", "gy"),
            P("gy"),
            P("gy"),
            P("gx", "gy"),
        ),
        out_specs=(P(None, None, "gx", "gy"), P(None, None, "gx", "gy")),
        check_vma=False,
    )
```

```python
import functools
import math

import jax
import jax.numpy as jnp
from jax import lax
from jax.experimental import pallas as pl
from jax.experimental.pallas import tpu as pltpu
from jax.sharding import PartitionSpec as P

ITERS = 2
LMAX = 4


ramp_rate = 0.7
decay_rate = 0.25
shade_scale = 0.1


def shifted(block, axis, distance):
    devices = range(lax.axis_size(axis))
    route = [(i, i + distance) for i in devices if i + distance in devices]
    return lax.ppermute(block, axis, route)


def vertical(field):
    zero = jnp.zeros((1,) + field.shape[1:], jnp.float32)
    upper = jnp.concatenate([field[1:], zero], axis=0)
    lower = jnp.concatenate([zero, field[:-1]], axis=0)
    return upper - lower


KPAD = 32


def rolled(a, shift, axis):
    shift %= a.shape[axis]
    return pltpu.roll(a, shift, axis) if shift else a


def pack_halos(levels, tile, to_xp, to_xm, to_yp, to_ym, only=None):
    nx, ny = to_yp.shape[1] // KPAD, to_xp.shape[2]
    row = lax.broadcasted_iota(jnp.int32, (nx, ny), 0)
    hi_x = (("p", nx - 2), ("p", nx - 1), ("u", nx - 1), ("th", nx - 1), ("q", nx - 1))
    lo_x = (("p", 1), ("p", 0), ("u", 0), ("th", 0), ("q", 0))
    hi_y = (("p", ny - 2), ("p", ny - 1), ("v", ny - 1), ("th", ny - 1), ("q", ny - 1))
    lo_y = (("p", 1), ("p", 0), ("v", 0), ("th", 0), ("q", 0))
    zero = jnp.zeros((nx, ny), jnp.float32)
    names = sorted({name for name, _ in hi_y + lo_y if only is None or name == "th"})
    flipped = {}
    for name in names:
        stacked = jnp.concatenate([tile(name, k) for k in range(levels)] + [zero] * (KPAD - levels), axis=0)
        flipped[name] = stacked.T
    for spec, to_y in ((hi_y, to_yp), (lo_y, to_ym)):
        for i, (name, c) in enumerate(spec):
            if only is not None and i != only:
                continue
            to_y[i : i + 1, :] = flipped[name][c : c + 1, :]
        if only is None:
            to_y[len(spec) :, :] = jnp.zeros((to_y.shape[0] - len(spec), to_y.shape[1]), jnp.float32)
    for spec, to_x in ((hi_x, to_xp), (lo_x, to_xm)):
        for i, (name, r) in enumerate(spec):
            if only is not None and i != only:
                continue
            for g in range(KPAD // nx):
                acc = zero
                for k in range(g * nx, min(levels, (g + 1) * nx)):
                    acc = jnp.where(row == k % nx, rolled(tile(name, k), k - r, 0), acc)
                to_x[i, g * nx : (g + 1) * nx, :] = acc


def state_tile(winds, thermo):
    refs = {"u": winds.at[0], "v": winds.at[1], "p": thermo.at[0], "th": thermo.at[1], "q": thermo.at[2]}
    return lambda name, k: refs[name][k]


def pack_kernel(terrain, winds, thermo, to_xp, to_xm, to_yp, to_ym):
    levels, nx = winds.shape[1], winds.shape[2]
    pack_halos(levels, state_tile(winds, thermo), to_xp, to_xm, to_yp, to_ym)
    ramp = ramp_rate * lax.broadcasted_iota(jnp.int32, terrain.shape, 0).astype(jnp.float32) / nx
    height = terrain[...]
    west = jnp.sum(jnp.exp(height + ramp) * (shade_scale / nx), axis=0, keepdims=True)
    east = jnp.sum(jnp.exp(height - ramp) * (shade_scale / nx), axis=0, keepdims=True)
    to_xp[0, levels : levels + 1, :] = west
    to_xm[0, levels : levels + 1, :] = east


def substep_kernel(devices, add_heat, *refs):
    if add_heat:
        profile, winds, thermo, heating = refs[:4]
        refs = refs[4:]
    else:
        winds, thermo = refs[:2]
        refs = refs[2:]
    from_xm, from_xp, from_ym, from_yp, winds_out, thermo_out = refs[:6]
    sends, y_halo = refs[6:-1], refs[-1]
    levels, nx, ny = winds.shape[1:]
    ix, iy = lax.axis_index("gx"), lax.axis_index("gy")
    edge = (ix == 0, ix == devices[0] - 1, iy == 0, iy == devices[1] - 1)
    row = lax.broadcasted_iota(jnp.int32, (nx, ny), 0)
    lane = lax.broadcasted_iota(jnp.int32, (nx, ny), 1)
    xm = lambda i, k: rolled(from_xm[i, (k // nx) * nx : (k // nx + 1) * nx, :], -k, 0)
    xp = lambda i, k: rolled(from_xp[i, (k // nx) * nx : (k // nx + 1) * nx, :], nx - 1 - k, 0)
    edge_row = lax.broadcasted_iota(jnp.int32, (ny, KPAD * nx), 0)
    for i in range(5):
        lo = jnp.broadcast_to(from_ym[i : i + 1, :], (ny, KPAD * nx))
        hi = jnp.broadcast_to(from_yp[i : i + 1, :], (ny, KPAD * nx))
        y_halo[i] = jnp.where(edge_row == 0, lo, jnp.where(edge_row == ny - 1, hi, 0.0)).T
    yh = lambda i, k: y_halo[i, k * nx : (k + 1) * nx, :]
    x_up = lambda f, h: jnp.where(row == nx - 1, h, pltpu.roll(f, nx - 1, 0))
    x_dn = lambda f, h: jnp.where(row == 0, h, pltpu.roll(f, 1, 0))
    y_up = lambda f, h: jnp.where(lane == ny - 1, h, pltpu.roll(f, ny - 1, 1))
    y_dn = lambda f, h: jnp.where(lane == 0, h, pltpu.roll(f, 1, 1))

    def vert(ref, k):
        upper = ref[k + 1] if k + 1 < levels else jnp.zeros((nx, ny), jnp.float32)
        lower = ref[k - 1] if k > 0 else jnp.zeros((nx, ny), jnp.float32)
        return upper - lower

    press = thermo.at[0]
    for k in range(levels):
        p = press[k]
        theta = thermo[1, k]
        winds_out[0, k] = winds[0, k] - 0.25 * (x_up(p, xp(1, k)) - x_dn(p, xm(1, k)))
        winds_out[1, k] = winds[1, k] - 0.25 * (y_up(p, yh(1, k)) - y_dn(p, yh(1, k)))
        up_n = winds[2, k] - 0.25 * vert(press, k) + 0.1 * theta
        winds_out[2, k] = up_n
        for index in (1, 2):
            field = thermo[index, k]
            east_c = x_up(field, xp(index + 2, k))
            west_c = x_dn(field, xm(index + 2, k))
            lap = east_c + west_c + y_up(field, yh(index + 2, k)) + y_dn(field, yh(index + 2, k)) - 4.0 * field
            new = field + 0.1 * lap - 0.15 * (east_c - west_c)
            if index == 1:
                new = new - 0.1 * up_n
                if add_heat:
                    new = new + profile[k] * heating[...]
            thermo_out[index, k] = new
    up_out = winds_out.at[2]
    for k in range(levels):
        p = press[k]
        east_hi = xp(2, k) - 0.25 * (xp(0, k) - p)
        east_lo = xm(2, k) - 0.25 * (p - xm(0, k))
        north_hi = yh(2, k) - 0.25 * (yh(0, k) - p)
        north_lo = yh(2, k) - 0.25 * (p - yh(0, k))
        east_hi = jnp.where(edge[1], 0.0, east_hi)
        east_lo = jnp.where(edge[0], 0.0, east_lo)
        north_hi = jnp.where(edge[3], 0.0, north_hi)
        north_lo = jnp.where(edge[2], 0.0, north_lo)
        east_n = winds_out[0, k]
        north_n = winds_out[1, k]
        diverge = (x_up(east_n, east_hi) - x_dn(east_n, east_lo)) + (
            y_up(north_n, north_hi) - y_dn(north_n, north_lo)
        )
        thermo_out[0, k] = p - 0.25 * (diverge + vert(up_out, k))
    if sends:
        pack_halos(levels, state_tile(winds_out, thermo_out), *sends)


def halo_shapes(winds):
    _, levels, nx, ny = winds.shape
    x_msg = jax.ShapeDtypeStruct((5, KPAD, ny), jnp.float32)
    y_msg = jax.ShapeDtypeStruct((8, KPAD * nx), jnp.float32)
    return (x_msg, x_msg, y_msg, y_msg)


VMEM = pl.BlockSpec(memory_space=pltpu.VMEM)


def pack(winds, thermo, tots):
    return pl.pallas_call(
        pack_kernel,
        out_shape=halo_shapes(winds),
        in_specs=[VMEM] * 3,
        out_specs=(VMEM,) * 4,
    )(tots, winds, thermo)


def heat_kernel(profile, shade, vecs, relay, thermo, xp_in, xm_in, yp_in, ym_in, thermo_out, to_xp, to_xm, to_yp, to_ym, heat_out):
    west_far = (vecs[0:1, :] + vecs[2:3, :] * relay[0:1, :]) + vecs[3:4, :] * relay[1:2, :]
    east_far = (vecs[1:2, :] + vecs[2:3, :] * relay[2:3, :]) + vecs[3:4, :] * relay[3:4, :]
    west_occ = (shade[0] + west_far) * shade[2]
    east_occ = (shade[1] + east_far) * shade[3]
    sun = jnp.where(vecs[4:5, :] != 0.0, 1.0 / (1.0 + west_occ), 1.0 / (1.0 + east_occ))
    sky = 1.0 / (1.0 + 0.5 * (west_occ + east_occ))
    land = vecs[5:6, :]
    heat_out[...] = land * (0.7 * sun + 0.3 * sky) + (1.0 - land) * 0.3 * sky
    heating = heat_out
    levels = thermo.shape[1]
    for k in range(levels):
        thermo_out[0, k] = thermo[0, k]
        thermo_out[2, k] = thermo[2, k]
        thermo_out[1, k] = thermo[1, k] + profile[k] * heating[...]
    for src, dst in ((xp_in, to_xp), (xm_in, to_xm), (yp_in, to_yp), (ym_in, to_ym)):
        for i in range(src.shape[0]):
            if i != 3:
                dst[i] = src[i]
    refs = {"th": thermo_out.at[1]}
    pack_halos(levels, lambda name, k: refs[name][k], to_xp, to_xm, to_yp, to_ym, only=3)


def add_heat(thermo, sends, profile, shade, vecs, relay):
    smem = pl.BlockSpec(memory_space=pltpu.SMEM)
    like = lambda a: jax.ShapeDtypeStruct(a.shape, jnp.float32)
    return pl.pallas_call(
        heat_kernel,
        out_shape=(like(thermo),) + tuple(like(m) for m in sends) + (like(shade[0]),),
        in_specs=[smem] + [VMEM] * 8,
        out_specs=(VMEM,) * 6,
    )(profile, shade, vecs, relay, thermo, *sends)


def substep(winds, thermo, halos, heat, emit):
    outs = (
        jax.ShapeDtypeStruct(winds.shape, jnp.float32),
        jax.ShapeDtypeStruct(thermo.shape, jnp.float32),
    )
    if emit:
        outs = outs + halo_shapes(winds)
    devices = (lax.axis_size("gx"), lax.axis_size("gy"))
    smem = pl.BlockSpec(memory_space=pltpu.SMEM)
    heat_args = (heat[0], winds, thermo, heat[1]) if heat else (winds, thermo)
    heat_specs = [smem, VMEM, VMEM, VMEM] if heat else [VMEM, VMEM]
    return pl.pallas_call(
        functools.partial(substep_kernel, devices, bool(heat)),
        out_shape=outs,
        in_specs=heat_specs + [VMEM] * 4,
        out_specs=(VMEM,) * len(outs),
        scratch_shapes=[pltpu.VMEM((5, KPAD * winds.shape[2], winds.shape[3]), jnp.float32)],
    )(*heat_args, *halos)


def per_device(winds, thermo, terrain, shadow_len, sector, land_mask):
    cols_x, cols_y = terrain.shape
    levels = winds.shape[1]
    ramp = (ramp_rate * jnp.arange(cols_x).astype(jnp.float32) / cols_x)[:, None]
    west_terms = jnp.exp(terrain + ramp) * (shade_scale / cols_x)
    east_terms = jnp.exp(terrain - ramp) * (shade_scale / cols_x)
    prefix = jnp.cumsum(west_terms, axis=0) - west_terms
    east_tot = jnp.sum(east_terms, axis=0)
    suffix = east_tot[None, :] - jnp.cumsum(east_terms, axis=0)

    to_xp, to_xm, to_yp, to_ym = pack(winds, thermo, terrain)
    far = {}
    for step in range(ITERS):
        from_xm = shifted(to_xp, "gx", 1)
        from_xp = shifted(to_xm, "gx", -1)
        from_ym = shifted(to_yp, "gy", 1)
        from_yp = shifted(to_ym, "gy", -1)
        if step == 0:
            near_w = shifted(to_xp[0, levels], "gx", 2)
            near_e = shifted(to_xm[0, levels], "gx", -2)
            far[("w", 1)] = from_xm[0, levels]
            far[("e", 1)] = from_xp[0, levels]
            far[("w", 2)] = near_w
            far[("e", 2)] = near_e
            relay_w = shifted(jnp.stack([far[("w", 1)], near_w]), "gx", 2)
            relay_e = shifted(jnp.stack([far[("e", 1)], near_e]), "gx", -2)
            far[("w", 3)], far[("w", 4)] = relay_w[0], relay_w[1]
            far[("e", 3)], far[("e", 4)] = relay_e[0], relay_e[1]
            west_near = jnp.zeros((cols_y,), jnp.float32)
            east_near = jnp.zeros((cols_y,), jnp.float32)
            weights = [jnp.where(shadow_len >= reach, math.exp(-decay_rate * reach), 0.0) for reach in range(1, LMAX + 1)]
            for reach in (1, 2):
                west_near = west_near + weights[reach - 1] * far[("w", reach)]
                east_near = east_near + weights[reach - 1] * far[("e", reach)]
            land = land_mask[0, 0].astype(jnp.float32)
            shade = jnp.stack([prefix, suffix, jnp.exp(-terrain - ramp), jnp.exp(ramp - terrain)])
            vecs = jnp.stack(
                [west_near, east_near, weights[2], weights[3], (sector == 0).astype(jnp.float32)]
                + [jnp.full((cols_y,), land)] + [jnp.zeros((cols_y,), jnp.float32)] * 2
            )
            relay = jnp.concatenate([relay_w, relay_e])
            profile = jnp.exp(-jnp.arange(levels).astype(jnp.float32) / 4.0)
        halos = (from_xm, from_xp, from_ym, from_yp)
        emit = step + 1 < ITERS
        outs = substep(winds, thermo, halos, () if step == 0 else (profile, heating), emit)
        winds, thermo = outs[0], outs[1]
        if step == 0:
            thermo, *sends, heating = add_heat(thermo, outs[2:], profile, shade, vecs, relay)
        if emit:
            to_xp, to_xm, to_yp, to_ym = sends
    return (winds, thermo)


def solution(mesh):
    return jax.shard_map(
        per_device,
        mesh=mesh,
        in_specs=(
            P(None, None, "gx", "gy"),
            P(None, None, "gx", "gy"),
            P("gx", "gy"),
            P("gy"),
            P("gy"),
            P("gx", "gy"),
        ),
        out_specs=(P(None, None, "gx", "gy"), P(None, None, "gx", "gy")),
        check_vma=False,
    )
```
